256 devices in a mesh: tile: 64 (over x, z, core), row: 4 (over y).
Axes of the slice: x: 4, y: 4, z: 8, core: 2. Of those that a mesh axis runs over, the one named last changes fastest.
Arguments:
- amplitudes: float32 [576, 64, 256], P('tile'), may hold values from -6 to 6
- integrals: float32 [4, 4096, 128, 256], P('row', 'tile'), may hold values from -0.0390625 to 0.0390625
- slot_ab: int32 [4, 4096], P('row', 'tile'), may hold values from 0 to 17
- slot_cd: int32 [4, 4096], P('row', 'tile'), may hold values from 0 to 575, as said below
- live_count: int32 [4, 64], P('row', 'tile'), may hold values from 1 to 64, as said below
- pair_list: int32 [64, 2], replicated, may hold values from 0 to 127, as said below
Outputs:
- symmetrized: float32 [64, 96, 96], P('tile', 'row')
The draws below stay inside these ranges and needn't reach their ends.
Inputs may be any that keep to these rules, and one draw needn't show every extreme that they name: `slot_cd`: slot s of row index r belongs to tile index k = s // 64; its cd tile is held in amplitudes by tile index k - 1, k or k + 1, taken cyclically over the tile axis (cd tile c is held by tile index c // 9). `live_count`: slots at or after a device's count are unused. In every row index some device uses all 64 slots. `pair_list`: the rows are distinct pairs (i, j) with i != j, and for every row the reversed pair (j, i) is also a row.
All inputs are finite; a program needn't handle non-finite values.
Results may differ from the reference program's by a relative error of at most 0.0003.
Values sent between devices are 32-bit elements; how exact they have to be, the bound alone decides.
No kernel may reach another device: no remote copies, remote signals or barrier semaphores. Data moves between devices by JAX's collectives and lax.ppermute only.
A program may use at most 64 MiB of HBM per device.

```python
import jax
import jax.numpy as jnp
from jax import lax

NOCC = 128
TS = 16
ATS = 8
SLAB = 96
PAIRS = 64
KCAP = 64
TW = 256
ABW = 128
CDT = 576
CDT_DEV = 9
ABT_ROW = 18
SLOTS = 4096
N_TILE = 64
N_ROW = 4


def draw_slot_cd(key, part):
    drawn = jax.random.randint(jax.random.fold_in(key, 11), (N_ROW, N_TILE * KCAP), 0, 3 * CDT_DEV)
    owners = jnp.arange(N_TILE * KCAP, dtype=jnp.int32) // KCAP
    owner_tile = (owners[None, :] + drawn // CDT_DEV + N_TILE - 1) % N_TILE
    return (owner_tile * CDT_DEV + drawn % CDT_DEV).astype(jnp.int32)


def draw_live_count(key, part):
    key_base, key_heavy, key_pick, key_top = jax.random.split(jax.random.fold_in(key, 23), 4)
    base_count = jax.random.randint(key_base, (N_ROW, N_TILE), max(1, KCAP // 8), KCAP // 2 + 1)
    heavy_count = jax.random.randint(key_heavy, (N_ROW, N_TILE), 3 * KCAP // 4, KCAP + 1)
    picked = jax.random.randint(key_pick, (N_ROW, N_TILE), 0, 8) == 0
    busiest = jax.random.randint(key_top, (N_ROW, 1), 0, N_TILE)
    counts = jnp.where(picked, heavy_count, base_count)
    counts = jnp.where(jnp.arange(N_TILE, dtype=jnp.int32)[None, :] == busiest, KCAP, counts)
    return counts.astype(jnp.int32)


def draw_pair_list(key, part):
    key_orbs, key_rows = jax.random.split(jax.random.fold_in(key, 37))
    shuffled = jax.random.permutation(key_orbs, NOCC)
    half_count = PAIRS // 2
    first_orb = shuffled[:half_count]
    second = shuffled[half_count:PAIRS]
    listed = jnp.concatenate([jnp.stack([first_orb, second], axis=1), jnp.stack([second, first_orb], axis=1)], axis=0)
    reorder = jax.random.permutation(key_rows, PAIRS)
    return jnp.take(listed, reorder, axis=0).astype(jnp.int32)


def with_ends(values, key, least, top_value):
    index_at = [jax.random.randint(jax.random.fold_in(key, axis), (), 0, length) for axis, length in enumerate(values.shape)]
    main_axis = values.shape.index(max(values.shape))
    neighbour = index_at[:main_axis] + [(index_at[main_axis] + 1) % values.shape[main_axis]] + index_at[main_axis + 1:]
    return values.at[tuple(index_at)].set(least).at[tuple(neighbour)].set(top_value)


def level_of(stream_key, extent, cuts, least, largest):
    factor_of = 1.0
    for axis_at, shards_of in cuts:
        steps = jax.random.uniform(jax.random.fold_in(jax.random.fold_in(stream_key, 6), axis_at), (shards_of,), jnp.float32, least / len(cuts), largest / len(cuts))
        factor_of = factor_of * jnp.repeat(jnp.exp(steps), extent[axis_at] // shards_of).reshape((-1,) + (1,) * (len(extent) - 1 - axis_at))
    return factor_of


def noise(stream_key, dims, scale, reach, shards=(), held_as=jnp.bfloat16):
    array = jax.random.normal(stream_key, dims, jnp.float32) * scale
    if len(shards) > 0:
        array = level_of(stream_key, dims, shards, -0.22, 0.18) * array
    return jnp.clip(array, min=-reach, max=reach).astype(held_as)


def setup_inputs(seed: int = 0) -> dict:
    key_of = jax.random.split(jax.random.key(seed), 7)
    amplitudes = noise(key_of[0], (CDT, PAIRS, TW), 1.0, 6.0, ((0, 64),), jnp.float32)
    integrals = noise(key_of[1], (N_ROW, SLOTS, ABW, TW), (TW * N_TILE * KCAP // (3 * ABT_ROW)) ** -0.5, 0.0390625, ((0, 4), (1, 64)), jnp.float32)
    slot_ab = with_ends(jax.random.randint(key_of[2], (N_ROW, SLOTS), 0, ABT_ROW), jax.random.fold_in(key_of[2], 1), 0, ABT_ROW - 1).astype(jnp.int32)
    slot_cd = draw_slot_cd(jax.random.fold_in(key_of[6], 71), 0)
    live_count = draw_live_count(jax.random.fold_in(key_of[6], 71), 0)
    pair_list = draw_pair_list(jax.random.fold_in(key_of[6], 71), 0)
    return {"amplitudes": amplitudes, "integrals": integrals, "slot_ab": slot_ab, "slot_cd": slot_cd, "live_count": live_count, "pair_list": pair_list}


def find_mirror(pair_list):
    first_orb = pair_list[:, 0]
    second = pair_list[:, 1]
    matches = (first_orb[:, None] == second[None, :]) & (second[:, None] == first_orb[None, :])
    columns = jnp.arange(pair_list.shape[0], dtype=jnp.int32)
    return jnp.sum(jnp.where(matches, columns[None, :], 0), axis=1).astype(jnp.int32)


def to_grid(totals, a_tiles, b_tiles):
    pair_count = totals.shape[1]
    shaped = totals.reshape(a_tiles, b_tiles, pair_count, ATS, TS)
    return jnp.transpose(shaped, (2, 0, 3, 1, 4)).reshape(pair_count, a_tiles * ATS, b_tiles * TS)


def reference(amplitudes, integrals, slot_ab, slot_cd, live_count, pair_list):
    highest = lax.Precision.HIGHEST
    a_tiles = SLAB // (N_ROW * ATS)
    b_tiles = SLAB // TS
    tiles_ab = a_tiles * b_tiles
    slices = []
    for row_index in range(N_ROW):
        def per_owner(totals, owner_index, row_index=row_index):
            first_slot = (owner_index * KCAP).astype(jnp.int32)
            cd_tiles = lax.dynamic_slice_in_dim(slot_cd[row_index], first_slot, KCAP)
            ab_tiles = lax.dynamic_slice_in_dim(slot_ab[row_index], first_slot, KCAP)
            blocks = lax.dynamic_slice_in_dim(integrals[row_index], first_slot, KCAP, 0)
            live_mask = (jnp.arange(KCAP, dtype=jnp.int32) < live_count[row_index, owner_index]).astype(jnp.float32)
            amp_tiles = jnp.take(amplitudes, cd_tiles, axis=0)
            products = jnp.einsum("spw,sbw->spb", amp_tiles, blocks, precision=highest)
            one_hot = (ab_tiles[:, None] == jnp.arange(tiles_ab, dtype=jnp.int32)[None, :]).astype(jnp.float32) * live_mask[:, None]
            return totals + jnp.einsum("se,spb->epb", one_hot, products, precision=highest), None

        start_totals = jnp.zeros((tiles_ab, PAIRS, ATS * TS), jnp.float32)
        totals, unused = lax.scan(per_owner, start_totals, jnp.arange(N_TILE, dtype=jnp.int32))
        slices.append(to_grid(totals, a_tiles, b_tiles))
    ladder = jnp.concatenate(slices, axis=1)
    mirrored = jnp.take(ladder, find_mirror(pair_list), axis=0)
    return ladder + jnp.transpose(mirrored, (0, 2, 1))
```

```python
import jax
import jax.numpy as jnp
from jax import lax
from jax.sharding import Mesh, PartitionSpec as P

TS = 16
ATS = 8
SLAB = 96


def padded(x, sides, width):
    for axis, dim in sides:
        size, length = (lax.axis_size(axis), x.shape[dim])
        up = [(i, (i + 1) % size) for i in range(size)]
        down = [(j, i) for i, j in up]
        last = lax.slice_in_dim(x, length - width, length, axis=dim)
        first = lax.slice_in_dim(x, 0, width, axis=dim)
        before = lax.ppermute(last, axis, up)
        after = lax.ppermute(first, axis, down)
        x = jnp.concatenate([before, x, after], axis=dim)
    return x


def find_mirror(pair_list):
    first_orb = pair_list[:, 0]
    second = pair_list[:, 1]
    matches = (first_orb[:, None] == second[None, :]) & (second[:, None] == first_orb[None, :])
    columns = jnp.arange(pair_list.shape[0], dtype=jnp.int32)
    return jnp.sum(jnp.where(matches, columns[None, :], 0), axis=1)


def to_grid(totals, a_tiles, b_tiles):
    pair_count = totals.shape[1]
    shaped = totals.reshape(a_tiles, b_tiles, pair_count, ATS, TS)
    return jnp.transpose(shaped, (2, 0, 3, 1, 4)).reshape(pair_count, a_tiles * ATS, b_tiles * TS)


def shards(amplitudes, integrals, slot_ab, slot_cd, live_count, pair_list):
    highest = lax.Precision.HIGHEST
    tile_size = lax.axis_size(TILE)
    row_size = lax.axis_size("row")
    tile_index = lax.axis_index(TILE)
    shard_tiles = amplitudes.shape[0]
    pair_count = amplitudes.shape[1]
    extended = padded(amplitudes, ((TILE, 0),), shard_tiles)
    blocks_all = integrals[0]
    ab_local = slot_ab[0]
    cd_global = slot_cd[0]
    owner_tile = cd_global // shard_tiles
    offset = (owner_tile - tile_index + 1 + tile_size) % tile_size
    ext_index = offset * shard_tiles + cd_global % shard_tiles
    live_total = live_count[0, 0]
    a_tiles = SLAB // (row_size * ATS)
    b_tiles = SLAB // TS
    tiles_ab = a_tiles * b_tiles
    block_width = integrals.shape[2]
    group_size = 8

    def block_step(block_index, totals):
        first_slot = block_index * group_size
        picked = lax.dynamic_slice_in_dim(ext_index, first_slot, group_size)
        ab_tiles = lax.dynamic_slice_in_dim(ab_local, first_slot, group_size)
        blocks = lax.dynamic_slice_in_dim(blocks_all, first_slot, group_size, 0)
        live_mask = (first_slot + jnp.arange(group_size, dtype=jnp.int32) < live_total).astype(
            jnp.float32
        )
        amp_tiles = jnp.take(extended, picked, axis=0)
        products = jnp.einsum(
            "spw,sbw->spb", amp_tiles, blocks, precision=highest, preferred_element_type=jnp.float32
        )
        one_hot = (ab_tiles[:, None] == jnp.arange(tiles_ab, dtype=jnp.int32)[None, :]).astype(
            jnp.float32
        ) * live_mask[:, None]
        return totals + jnp.einsum(
            "se,spb->epb", one_hot, products, precision=highest, preferred_element_type=jnp.float32
        )

    turn_count = (live_total + group_size - 1) // group_size
    start_totals = jnp.zeros((tiles_ab, pair_count, block_width), jnp.float32)
    totals = lax.fori_loop(0, turn_count, block_step, start_totals)
    whole_term = to_grid(totals, a_tiles, b_tiles)
    mirror = find_mirror(pair_list)
    mirrored = jnp.take(whole_term, mirror, axis=0)
    both = jnp.stack([whole_term, mirrored], axis=1)
    reduced = reduce_over_tile(both)
    own = reduced[:, 0]
    exchanged = lax.all_to_all(reduced[:, 1], "row", split_axis=2, concat_axis=1, tiled=True)
    turned = jnp.transpose(exchanged, (0, 2, 1))
    return own + turned


def reduce_over_tile(x):
    chips = lax.axis_size(CHIPS)
    cores = lax.axis_size("c")
    shaped = x.reshape((chips, cores) + x.shape[1:])
    core = lax.axis_index("c")
    mine = jnp.take(shaped, core, axis=1)
    other = jnp.take(shaped, 1 - core, axis=1)
    summed = mine + lax.ppermute(other, "c", [(0, 1), (1, 0)])
    spread = lax.all_to_all(summed, CHIPS, 0, 0, tiled=True)
    return jnp.sum(spread, axis=0, keepdims=True)


CHIPS = ("x", "z")
TILE = ("x", "z", "c")


def solution(mesh):
    tile_size = mesh.shape["tile"]
    row_size = mesh.shape["row"]
    cores = 2
    split = Mesh(
        mesh.devices.reshape(4, tile_size // (4 * cores), cores, row_size), ("x", "z", "c", "row")
    )
    return jax.shard_map(
        shards,
        mesh=split,
        in_specs=(
            P(TILE, None, None),
            P("row", TILE, None, None),
            P("row", TILE),
            P("row", TILE),
            P("row", TILE),
            P(),
        ),
        out_specs=P(TILE, "row", None),
        check_vma=False,
    )
```

```python
import functools

import jax
import jax.numpy as jnp
from jax import lax
from jax.experimental import pallas as pl
from jax.experimental.pallas import tpu as pltpu
from jax.sharding import Mesh, PartitionSpec as P

TS = 16
ATS = 8
SLAB = 96
GROUP = 8
CHIPS = ("x", "z")
TILE = ("x", "z", "c")


def padded(x, sides, width):
    for axis, dim in sides:
        size, length = (lax.axis_size(axis), x.shape[dim])
        up = [(i, (i + 1) % size) for i in range(size)]
        down = [(j, i) for i, j in up]
        last = lax.slice_in_dim(x, length - width, length, axis=dim)
        first = lax.slice_in_dim(x, 0, width, axis=dim)
        before = lax.ppermute(last, axis, up)
        after = lax.ppermute(first, axis, down)
        x = jnp.concatenate([before, x, after], axis=dim)
    return x


def find_mirror(pair_list):
    first_orb = pair_list[:, 0]
    second = pair_list[:, 1]
    matches = (first_orb[:, None] == second[None, :]) & (second[:, None] == first_orb[None, :])
    columns = jnp.arange(pair_list.shape[0], dtype=jnp.int32)
    return jnp.sum(jnp.where(matches, columns[None, :], 0), axis=1)


def to_grid(totals, a_tiles, b_tiles):
    pair_count = totals.shape[1]
    shaped = totals.reshape(a_tiles, b_tiles, pair_count, ATS, TS)
    return jnp.transpose(shaped, (2, 0, 3, 1, 4)).reshape(pair_count, a_tiles * ATS, b_tiles * TS)


def slot_kernel(picked_ref, ab_ref, live_ref, amp_ref, block_ref, out_ref):
    step = pl.program_id(0)

    @pl.when(step == 0)
    def _():
        out_ref[...] = jnp.zeros_like(out_ref)

    for j in range(GROUP):
        slot = step * GROUP + j

        @pl.when(slot < live_ref[0])
        def _():
            amp = amp_ref[picked_ref[slot]]
            product = lax.dot_general(
                amp,
                block_ref[j],
                (((1,), (1,)), ((), ())),
                precision=lax.Precision.HIGHEST,
                preferred_element_type=jnp.float32,
            )
            target = ab_ref[slot]
            out_ref[target] = out_ref[target] + product


def slot_products(picked, ab_local, live, amps, blocks, tiles_ab):
    slots, block_width, width = blocks.shape
    rows = amps.shape[1]
    steps = slots // GROUP

    def block_map(i, picked_ref, ab_ref, live_ref):
        last = jnp.maximum(live_ref[0] - 1, 0) // GROUP
        return (jnp.minimum(i, last), 0, 0)

    grid_spec = pltpu.PrefetchScalarGridSpec(
        num_scalar_prefetch=3,
        grid=(steps,),
        in_specs=[
            pl.BlockSpec(amps.shape, lambda i, *_: (0, 0, 0)),
            pl.BlockSpec((GROUP, block_width, width), block_map),
        ],
        out_specs=pl.BlockSpec((tiles_ab, rows, block_width), lambda i, *_: (0, 0, 0)),
    )
    return pl.pallas_call(
        slot_kernel,
        grid_spec=grid_spec,
        out_shape=jax.ShapeDtypeStruct((tiles_ab, rows, block_width), jnp.float32),
        compiler_params=pltpu.CompilerParams(
            dimension_semantics=("arbitrary",), vmem_limit_bytes=48 * 1024 * 1024
        ),
        cost_estimate=pl.CostEstimate(
            flops=2 * slots * rows * width * block_width * 6,
            bytes_accessed=4 * (slots * block_width * width + amps.size + tiles_ab * rows * block_width),
            transcendentals=0,
        ),
    )(picked, ab_local, live, amps, blocks)


def reduce_over_tile(x):
    chips = lax.axis_size(CHIPS)
    cores = lax.axis_size("c")
    shaped = x.reshape(x.shape[:2] + (chips, cores) + x.shape[3:])
    core = lax.axis_index("c")
    mine = jnp.take(shaped, core, axis=3)
    other = jnp.take(shaped, 1 - core, axis=3)
    summed = mine + lax.ppermute(other, "c", [(0, 1), (1, 0)])
    spread = lax.all_to_all(summed, CHIPS, 2, 2, tiled=True)
    return jnp.sum(spread, axis=2)


def shards(amplitudes, integrals, slot_ab, slot_cd, live_count, pair_list):
    tile_size = lax.axis_size(TILE)
    row_size = lax.axis_size("row")
    tile_index = lax.axis_index(TILE)
    shard_tiles = amplitudes.shape[0]
    extended = padded(amplitudes, ((TILE, 0),), shard_tiles)
    mirror = find_mirror(pair_list)
    both = jnp.concatenate([extended, jnp.take(extended, mirror, axis=1)], axis=1)
    cd_global = slot_cd[0]
    owner_tile = cd_global // shard_tiles
    offset = (owner_tile - tile_index + 1 + tile_size) % tile_size
    ext_index = offset * shard_tiles + cd_global % shard_tiles
    a_tiles = SLAB // (row_size * ATS)
    b_tiles = SLAB // TS
    tiles_ab = a_tiles * b_tiles
    totals = slot_products(
        ext_index.astype(jnp.int32),
        slot_ab[0],
        live_count[0],
        both,
        integrals[0],
        tiles_ab,
    )
    pair_count = amplitudes.shape[1]
    halves = totals.reshape(tiles_ab, 2, pair_count, totals.shape[2])
    reduced = reduce_over_tile(halves)
    own = to_grid(reduced[:, 0][:, None], a_tiles, b_tiles)
    mirrored = to_grid(reduced[:, 1][:, None], a_tiles, b_tiles)
    exchanged = lax.all_to_all(mirrored, "row", split_axis=2, concat_axis=1, tiled=True)
    turned = jnp.transpose(exchanged, (0, 2, 1))
    return own + turned


def solution(mesh):
    tile_size = mesh.shape["tile"]
    row_size = mesh.shape["row"]
    cores = 2
    split = Mesh(
        mesh.devices.reshape(4, tile_size // (4 * cores), cores, row_size), ("x", "z", "c", "row")
    )
    return jax.shard_map(
        shards,
        mesh=split,
        in_specs=(
            P(TILE, None, None),
            P("row", TILE, None, None),
            P("row", TILE),
            P("row", TILE),
            P("row", TILE),
            P(),
        ),
        out_specs=P(TILE, "row", None),
        check_vma=False,
    )
```

```python
import functools

import jax
import jax.numpy as jnp
from jax import lax
from jax.experimental import pallas as pl
from jax.experimental.pallas import tpu as pltpu
from jax.sharding import Mesh, PartitionSpec as P

TS = 16
ATS = 8
SLAB = 96
GROUP = 8
CHIPS = ("x", "z")
TILE = ("x", "z", "c")


def padded(x, sides, width):
    for axis, dim in sides:
        size, length = (lax.axis_size(axis), x.shape[dim])
        up = [(i, (i + 1) % size) for i in range(size)]
        down = [(j, i) for i, j in up]
        last = lax.slice_in_dim(x, length - width, length, axis=dim)
        first = lax.slice_in_dim(x, 0, width, axis=dim)
        before = lax.ppermute(last, axis, up)
        after = lax.ppermute(first, axis, down)
        x = jnp.concatenate([before, x, after], axis=dim)
    return x


def find_mirror(pair_list):
    first_orb = pair_list[:, 0]
    second = pair_list[:, 1]
    matches = (first_orb[:, None] == second[None, :]) & (second[:, None] == first_orb[None, :])
    columns = jnp.arange(pair_list.shape[0], dtype=jnp.int32)
    return jnp.sum(jnp.where(matches, columns[None, :], 0), axis=1)


def to_grid(totals, a_tiles, b_tiles):
    pair_count = totals.shape[1]
    shaped = totals.reshape(a_tiles, b_tiles, pair_count, ATS, TS)
    return jnp.transpose(shaped, (2, 0, 3, 1, 4)).reshape(pair_count, a_tiles * ATS, b_tiles * TS)


def slot_kernel(offset_ref, local_ref, ab_ref, live_ref, before_ref, own_ref, after_ref,
                block_ref, perm_ref, mine_ref, other_ref, acc_ref):
    step = pl.program_id(0)

    @pl.when(step == 0)
    def _():
        acc_ref[...] = jnp.zeros_like(acc_ref)

    for j in range(GROUP):
        slot = step * GROUP + j
        for side, amp_ref in enumerate((before_ref, own_ref, after_ref)):

            @pl.when((slot < live_ref[0]) & (offset_ref[slot] == side))
            def _():
                product = lax.dot_general(
                    amp_ref[local_ref[slot]],
                    block_ref[j],
                    (((1,), (1,)), ((), ())),
                    precision=lax.Precision.HIGHEST,
                    preferred_element_type=jnp.float32,
                )
                target = ab_ref[slot]
                acc_ref[target] = acc_ref[target] + product

    @pl.when(step == pl.num_programs(0) - 1)
    def _():
        half = mine_ref.shape[1]
        for e in range(acc_ref.shape[0]):
            placed = jnp.dot(
                perm_ref[...], acc_ref[e], precision=lax.Precision.HIGHEST,
                preferred_element_type=jnp.float32,
            )
            mine_ref[e] = placed[:half]
            other_ref[e] = placed[half:]


def slot_products(offset, local, ab_local, live, before, own, after, blocks, perm, tiles_ab):
    slots, block_width, width = blocks.shape
    pairs = own.shape[1]
    steps = slots // GROUP

    def block_map(i, *refs):
        last = jnp.maximum(refs[3][0] - 1, 0) // GROUP
        return (jnp.minimum(i, last), 0, 0)

    whole = lambda shape: pl.BlockSpec(shape, lambda i, *_: (0,) * len(shape))
    out_shape = (tiles_ab, perm.shape[0] // 2, block_width)
    grid_spec = pltpu.PrefetchScalarGridSpec(
        num_scalar_prefetch=4,
        grid=(steps,),
        in_specs=[
            whole(before.shape),
            whole(own.shape),
            whole(after.shape),
            pl.BlockSpec((GROUP, block_width, width), block_map),
            whole(perm.shape),
        ],
        out_specs=[whole(out_shape), whole(out_shape)],
        scratch_shapes=[pltpu.VMEM((tiles_ab, pairs, block_width), jnp.float32)],
    )
    return pl.pallas_call(
        slot_kernel,
        grid_spec=grid_spec,
        out_shape=[jax.ShapeDtypeStruct(out_shape, jnp.float32)] * 2,
        compiler_params=pltpu.CompilerParams(
            dimension_semantics=("arbitrary",), vmem_limit_bytes=48 * 1024 * 1024
        ),
        cost_estimate=pl.CostEstimate(
            flops=2 * slots * pairs * width * block_width * 6,
            bytes_accessed=4 * (slots * block_width * width + 3 * own.size + 2 * tiles_ab * pairs * block_width),
            transcendentals=0,
        ),
    )(offset, local, ab_local, live, before, own, after, blocks, perm)


def exchange_rows(mirrored):
    size = lax.axis_size("row")
    index = lax.axis_index("row")
    width = mirrored.shape[1]
    placed = jnp.zeros((1, size * width, width), mirrored.dtype)
    for shift in range(size):
        block = lax.dynamic_slice_in_dim(mirrored, ((index + shift) % size) * width, width, axis=2)
        if shift:
            block = lax.ppermute(block, "row", [(i, (i + shift) % size) for i in range(size)])
        source = (index - shift + size) % size
        placed = lax.dynamic_update_slice_in_dim(placed, block, source * width, axis=1)
    return placed


def shards(amplitudes, integrals, slot_ab, slot_cd, live_count, pair_list):
    tile_size = lax.axis_size(TILE)
    row_size = lax.axis_size("row")
    tile_index = lax.axis_index(TILE)
    core = lax.axis_index("c")
    cores = lax.axis_size("c")
    shard_tiles = amplitudes.shape[0]
    pair_count = amplitudes.shape[1]
    up = [(i, (i + 1) % tile_size) for i in range(tile_size)]
    down = [(j, i) for i, j in up]
    before = lax.ppermute(amplitudes, TILE, up)
    after = lax.ppermute(amplitudes, TILE, down)
    mirror = find_mirror(pair_list)
    chips_of = jnp.arange(pair_count // cores, dtype=jnp.int32) * cores
    kept = chips_of + core
    sent = chips_of + (cores - 1 - core)
    source = jnp.concatenate([kept, mirror[kept], sent, mirror[sent]])
    perm = (source[:, None] == jnp.arange(pair_count, dtype=jnp.int32)[None, :]).astype(jnp.float32)
    cd_global = slot_cd[0]
    owner_tile = cd_global // shard_tiles
    offset = (owner_tile - tile_index + 1 + tile_size) % tile_size
    a_tiles = SLAB // (row_size * ATS)
    b_tiles = SLAB // TS
    tiles_ab = a_tiles * b_tiles
    mine, other = slot_products(
        offset.astype(jnp.int32),
        (cd_global % shard_tiles).astype(jnp.int32),
        slot_ab[0],
        live_count[0],
        before,
        amplitudes,
        after,
        integrals[0],
        perm,
        tiles_ab,
    )
    summed = mine + lax.ppermute(other, "c", [(0, 1), (1, 0)])
    halves = summed.reshape(tiles_ab, 2, pair_count // cores, summed.shape[2])
    spread = lax.all_to_all(halves, CHIPS, 2, 2, tiled=True)
    reduced = jnp.sum(spread, axis=2)
    own = to_grid(reduced[:, 0][:, None], a_tiles, b_tiles)
    mirrored = to_grid(reduced[:, 1][:, None], a_tiles, b_tiles)
    turned = jnp.transpose(exchange_rows(mirrored), (0, 2, 1))
    return own + turned


def solution(mesh):
    tile_size = mesh.shape["tile"]
    row_size = mesh.shape["row"]
    cores = 2
    split = Mesh(
        mesh.devices.reshape(4, tile_size // (4 * cores), cores, row_size), ("x", "z", "c", "row")
    )
    return jax.shard_map(
        shards,
        mesh=split,
        in_specs=(
            P(TILE, None, None),
            P("row", TILE, None, None),
            P("row", TILE),
            P("row", TILE),
            P("row", TILE),
            P(),
        ),
        out_specs=P(TILE, "row", None),
        check_vma=False,
    )
```

```python
import functools

import jax
import jax.numpy as jnp
from jax import lax
from jax.experimental import pallas as pl
from jax.experimental.pallas import tpu as pltpu
from jax.sharding import Mesh, PartitionSpec as P

TS = 16
ATS = 8
SLAB = 96
GROUP = 8
CHIPS = ("x", "z")
TILE = ("x", "z", "c")


def padded(x, sides, width):
    for axis, dim in sides:
        size, length = (lax.axis_size(axis), x.shape[dim])
        up = [(i, (i + 1) % size) for i in range(size)]
        down = [(j, i) for i, j in up]
        last = lax.slice_in_dim(x, length - width, length, axis=dim)
        first = lax.slice_in_dim(x, 0, width, axis=dim)
        before = lax.ppermute(last, axis, up)
        after = lax.ppermute(first, axis, down)
        x = jnp.concatenate([before, x, after], axis=dim)
    return x


def find_mirror(pair_list):
    first_orb = pair_list[:, 0]
    second = pair_list[:, 1]
    matches = (first_orb[:, None] == second[None, :]) & (second[:, None] == first_orb[None, :])
    columns = jnp.arange(pair_list.shape[0], dtype=jnp.int32)
    return jnp.sum(jnp.where(matches, columns[None, :], 0), axis=1)


def to_grid(totals, a_tiles, b_tiles):
    pair_count = totals.shape[1]
    shaped = totals.reshape(a_tiles, b_tiles, pair_count, ATS, TS)
    return jnp.transpose(shaped, (2, 0, 3, 1, 4)).reshape(pair_count, a_tiles * ATS, b_tiles * TS)


def slot_kernel(offset_ref, local_ref, ab_ref, live_ref, before_ref, own_ref, after_ref,
                block_ref, perm_ref, mine_ref, other_ref, acc_ref):
    step = pl.program_id(0)

    @pl.when(step == 0)
    def _():
        acc_ref[...] = jnp.zeros_like(acc_ref)

    for j in range(GROUP):
        slot = step * GROUP + j
        for side, amp_ref in enumerate((before_ref, own_ref, after_ref)):

            @pl.when((slot < live_ref[0]) & (offset_ref[slot] == side))
            def _():
                product = lax.dot_general(
                    amp_ref[local_ref[slot]],
                    block_ref[j],
                    (((1,), (1,)), ((), ())),
                    precision=lax.Precision.HIGH,
                    preferred_element_type=jnp.float32,
                )
                target = ab_ref[slot]
                acc_ref[target] = acc_ref[target] + product

    @pl.when(step == pl.num_programs(0) - 1)
    def _():
        half = mine_ref.shape[1]
        for e in range(acc_ref.shape[0]):
            placed = jnp.dot(
                perm_ref[...], acc_ref[e], precision=lax.Precision.HIGHEST,
                preferred_element_type=jnp.float32,
            )
            mine_ref[e] = placed[:half]
            other_ref[e] = placed[half:]


def slot_products(offset, local, ab_local, live, before, own, after, blocks, perm, tiles_ab):
    slots, block_width, width = blocks.shape
    pairs = own.shape[1]
    steps = slots // GROUP

    def block_map(i, *refs):
        last = jnp.maximum(refs[3][0] - 1, 0) // GROUP
        return (jnp.minimum(i, last), 0, 0)

    whole = lambda shape: pl.BlockSpec(shape, lambda i, *_: (0,) * len(shape))
    out_shape = (tiles_ab, perm.shape[0] // 2, block_width)
    grid_spec = pltpu.PrefetchScalarGridSpec(
        num_scalar_prefetch=4,
        grid=(steps,),
        in_specs=[
            whole(before.shape),
            whole(own.shape),
            whole(after.shape),
            pl.BlockSpec((GROUP, block_width, width), block_map),
            whole(perm.shape),
        ],
        out_specs=[whole(out_shape), whole(out_shape)],
        scratch_shapes=[pltpu.VMEM((tiles_ab, pairs, block_width), jnp.float32)],
    )
    return pl.pallas_call(
        slot_kernel,
        grid_spec=grid_spec,
        out_shape=[jax.ShapeDtypeStruct(out_shape, jnp.float32)] * 2,
        compiler_params=pltpu.CompilerParams(
            dimension_semantics=("arbitrary",), vmem_limit_bytes=48 * 1024 * 1024
        ),
        cost_estimate=pl.CostEstimate(
            flops=2 * slots * pairs * width * block_width * 6,
            bytes_accessed=4 * (slots * block_width * width + 3 * own.size + 2 * tiles_ab * pairs * block_width),
            transcendentals=0,
        ),
    )(offset, local, ab_local, live, before, own, after, blocks, perm)


def exchange_rows(mirrored):
    size = lax.axis_size("row")
    index = lax.axis_index("row")
    width = mirrored.shape[1]
    placed = jnp.zeros((1, size * width, width), mirrored.dtype)
    for shift in range(size):
        block = lax.dynamic_slice_in_dim(mirrored, ((index + shift) % size) * width, width, axis=2)
        if shift:
            block = lax.ppermute(block, "row", [(i, (i + shift) % size) for i in range(size)])
        source = (index - shift + size) % size
        placed = lax.dynamic_update_slice_in_dim(placed, block, source * width, axis=1)
    return placed


def shards(amplitudes, integrals, slot_ab, slot_cd, live_count, pair_list):
    tile_size = lax.axis_size(TILE)
    row_size = lax.axis_size("row")
    tile_index = lax.axis_index(TILE)
    core = lax.axis_index("c")
    cores = lax.axis_size("c")
    shard_tiles = amplitudes.shape[0]
    pair_count = amplitudes.shape[1]
    up = [(i, (i + 1) % tile_size) for i in range(tile_size)]
    down = [(j, i) for i, j in up]
    before = lax.ppermute(amplitudes, TILE, up)
    after = lax.ppermute(amplitudes, TILE, down)
    mirror = find_mirror(pair_list)
    chips_of = jnp.arange(pair_count // cores, dtype=jnp.int32) * cores
    kept = chips_of + core
    sent = chips_of + (cores - 1 - core)
    source = jnp.concatenate([kept, mirror[kept], sent, mirror[sent]])
    perm = (source[:, None] == jnp.arange(pair_count, dtype=jnp.int32)[None, :]).astype(jnp.float32)
    cd_global = slot_cd[0]
    owner_tile = cd_global // shard_tiles
    offset = (owner_tile - tile_index + 1 + tile_size) % tile_size
    a_tiles = SLAB // (row_size * ATS)
    b_tiles = SLAB // TS
    tiles_ab = a_tiles * b_tiles
    mine, other = slot_products(
        offset.astype(jnp.int32),
        (cd_global % shard_tiles).astype(jnp.int32),
        slot_ab[0],
        live_count[0],
        before,
        amplitudes,
        after,
        integrals[0],
        perm,
        tiles_ab,
    )
    summed = mine + lax.ppermute(other, "c", [(0, 1), (1, 0)])
    halves = summed.reshape(tiles_ab, 2, pair_count // cores, summed.shape[2])
    spread = lax.all_to_all(halves, CHIPS, 2, 2, tiled=True)
    reduced = jnp.sum(spread, axis=2)
    own = to_grid(reduced[:, 0][:, None], a_tiles, b_tiles)
    mirrored = to_grid(reduced[:, 1][:, None], a_tiles, b_tiles)
    turned = jnp.transpose(exchange_rows(mirrored), (0, 2, 1))
    return own + turned


def solution(mesh):
    tile_size = mesh.shape["tile"]
    row_size = mesh.shape["row"]
    cores = 2
    split = Mesh(
        mesh.devices.reshape(4, tile_size // (4 * cores), cores, row_size), ("x", "z", "c", "row")
    )
    return jax.shard_map(
        shards,
        mesh=split,
        in_specs=(
            P(TILE, None, None),
            P("row", TILE, None, None),
            P("row", TILE),
            P("row", TILE),
            P("row", TILE),
            P(),
        ),
        out_specs=P(TILE, "row", None),
        check_vma=False,
    )
```

```python
import functools

import jax
import jax.numpy as jnp
from jax import lax
from jax.experimental import pallas as pl
from jax.experimental.pallas import tpu as pltpu
from jax.sharding import Mesh, PartitionSpec as P

TS = 16
ATS = 8
SLAB = 96
GROUP = 8
CHIPS = ("x", "z")
TILE = ("x", "z", "c")


def padded(x, sides, width):
    for axis, dim in sides:
        size, length = (lax.axis_size(axis), x.shape[dim])
        up = [(i, (i + 1) % size) for i in range(size)]
        down = [(j, i) for i, j in up]
        last = lax.slice_in_dim(x, length - width, length, axis=dim)
        first = lax.slice_in_dim(x, 0, width, axis=dim)
        before = lax.ppermute(last, axis, up)
        after = lax.ppermute(first, axis, down)
        x = jnp.concatenate([before, x, after], axis=dim)
    return x


def find_mirror(pair_list):
    first_orb = pair_list[:, 0]
    second = pair_list[:, 1]
    matches = (first_orb[:, None] == second[None, :]) & (second[:, None] == first_orb[None, :])
    columns = jnp.arange(pair_list.shape[0], dtype=jnp.int32)
    return jnp.sum(jnp.where(matches, columns[None, :], 0), axis=1)


def to_grid(totals, a_tiles, b_tiles):
    pair_count = totals.shape[1]
    shaped = totals.reshape(a_tiles, b_tiles, pair_count, ATS, TS)
    return jnp.transpose(shaped, (2, 0, 3, 1, 4)).reshape(pair_count, a_tiles * ATS, b_tiles * TS)


def slot_kernel(picked_ref, ab_ref, live_ref, before_ref, own_ref, after_ref,
                block_ref, out_ref, amp_ref, acc_ref):
    step = pl.program_id(0)
    shard_tiles = own_ref.shape[0]

    @pl.when(step == 0)
    def _():
        acc_ref[...] = jnp.zeros_like(acc_ref)
        for side, source in enumerate((before_ref, own_ref, after_ref)):
            amp_ref[side * shard_tiles:(side + 1) * shard_tiles] = source[...]

    @pl.when(step * GROUP < live_ref[0])
    def _():
        for j in range(GROUP):
            slot = step * GROUP + j
            product = lax.dot_general(
                amp_ref[picked_ref[slot]],
                block_ref[j],
                (((1,), (1,)), ((), ())),
                precision=lax.Precision.HIGH,
                preferred_element_type=jnp.float32,
            )
            target = ab_ref[slot]
            used = slot < live_ref[0]
            acc_ref[target] = acc_ref[target] + jnp.where(used, product, 0.0)

    @pl.when(step == pl.num_programs(0) - 1)
    def _():
        out_ref[...] = acc_ref[...]


def slot_products(picked, ab_local, live, before, own, after, blocks, tiles_ab):
    slots, block_width, width = blocks.shape
    pairs = own.shape[1]
    steps = slots // GROUP

    def block_map(i, *refs):
        last = jnp.maximum(refs[2][0] - 1, 0) // GROUP
        return (jnp.minimum(i, last), 0, 0)

    whole = lambda shape: pl.BlockSpec(shape, lambda i, *_: (0,) * len(shape))
    out_shape = (tiles_ab, pairs, block_width)
    grid_spec = pltpu.PrefetchScalarGridSpec(
        num_scalar_prefetch=3,
        grid=(steps,),
        in_specs=[
            whole(before.shape),
            whole(own.shape),
            whole(after.shape),
            pl.BlockSpec((GROUP, block_width, width), block_map),
        ],
        out_specs=whole(out_shape),
        scratch_shapes=[
            pltpu.VMEM((3 * own.shape[0],) + own.shape[1:], jnp.float32),
            pltpu.VMEM((tiles_ab, pairs, block_width), jnp.float32),
        ],
    )
    return pl.pallas_call(
        slot_kernel,
        grid_spec=grid_spec,
        out_shape=jax.ShapeDtypeStruct(out_shape, jnp.float32),
        compiler_params=pltpu.CompilerParams(
            dimension_semantics=("arbitrary",), vmem_limit_bytes=48 * 1024 * 1024
        ),
        cost_estimate=pl.CostEstimate(
            flops=2 * slots * pairs * width * block_width * 3,
            bytes_accessed=4 * (slots * block_width * width + 3 * own.size + tiles_ab * pairs * block_width),
            transcendentals=0,
        ),
    )(picked, ab_local, live, before, own, after, blocks)


def exchange_rows(mirrored):
    size = lax.axis_size("row")
    index = lax.axis_index("row")
    width = mirrored.shape[1]
    placed = jnp.zeros((1, size * width, width), mirrored.dtype)
    for shift in range(size):
        block = lax.dynamic_slice_in_dim(mirrored, ((index + shift) % size) * width, width, axis=2)
        if shift:
            block = lax.ppermute(block, "row", [(i, (i + shift) % size) for i in range(size)])
        source = (index - shift + size) % size
        placed = lax.dynamic_update_slice_in_dim(placed, block, source * width, axis=1)
    return placed


def shards(amplitudes, integrals, slot_ab, slot_cd, live_count, pair_list):
    tile_size = lax.axis_size(TILE)
    row_size = lax.axis_size("row")
    tile_index = lax.axis_index(TILE)
    core = lax.axis_index("c")
    cores = lax.axis_size("c")
    shard_tiles = amplitudes.shape[0]
    pair_count = amplitudes.shape[1]
    up = [(i, (i + 1) % tile_size) for i in range(tile_size)]
    down = [(j, i) for i, j in up]
    before = lax.ppermute(amplitudes, TILE, up)
    after = lax.ppermute(amplitudes, TILE, down)
    mirror = find_mirror(pair_list)
    chips_of = jnp.arange(pair_count // cores, dtype=jnp.int32) * cores
    kept = chips_of + core
    sent = chips_of + (cores - 1 - core)
    keep_rows = jnp.concatenate([kept, mirror[kept]])
    send_rows = jnp.concatenate([sent, mirror[sent]])
    cd_global = slot_cd[0]
    owner_tile = cd_global // shard_tiles
    offset = (owner_tile - tile_index + 1 + tile_size) % tile_size
    a_tiles = SLAB // (row_size * ATS)
    b_tiles = SLAB // TS
    tiles_ab = a_tiles * b_tiles
    totals = slot_products(
        (offset * shard_tiles + cd_global % shard_tiles).astype(jnp.int32),
        slot_ab[0],
        live_count[0],
        before,
        amplitudes,
        after,
        integrals[0],
        tiles_ab,
    )
    mine = jnp.take(totals, keep_rows, axis=1)
    other = jnp.take(totals, send_rows, axis=1)
    summed = mine + lax.ppermute(other, "c", [(0, 1), (1, 0)])
    halves = summed.reshape(tiles_ab, 2, pair_count // cores, summed.shape[2])
    spread = lax.all_to_all(halves, CHIPS, 2, 2, tiled=True)
    reduced = jnp.sum(spread, axis=2)
    own = to_grid(reduced[:, 0][:, None], a_tiles, b_tiles)
    mirrored = to_grid(reduced[:, 1][:, None], a_tiles, b_tiles)
    turned = jnp.transpose(exchange_rows(mirrored), (0, 2, 1))
    return own + turned


def solution(mesh):
    tile_size = mesh.shape["tile"]
    row_size = mesh.shape["row"]
    cores = 2
    split = Mesh(
        mesh.devices.reshape(4, tile_size // (4 * cores), cores, row_size), ("x", "z", "c", "row")
    )
    return jax.shard_map(
        shards,
        mesh=split,
        in_specs=(
            P(TILE, None, None),
            P("row", TILE, None, None),
            P("row", TILE),
            P("row", TILE),
            P("row", TILE),
            P(),
        ),
        out_specs=P(TILE, "row", None),
        check_vma=False,
    )
```

```python
import functools

import jax
import jax.numpy as jnp
from jax import lax
from jax.experimental import pallas as pl
from jax.experimental.pallas import tpu as pltpu
from jax.sharding import Mesh, PartitionSpec as P

TS = 16
ATS = 8
SLAB = 96
GROUP = 16
CHIPS = ("x", "z")
TILE = ("x", "z", "c")


def padded(x, sides, width):
    for axis, dim in sides:
        size, length = (lax.axis_size(axis), x.shape[dim])
        up = [(i, (i + 1) % size) for i in range(size)]
        down = [(j, i) for i, j in up]
        last = lax.slice_in_dim(x, length - width, length, axis=dim)
        first = lax.slice_in_dim(x, 0, width, axis=dim)
        before = lax.ppermute(last, axis, up)
        after = lax.ppermute(first, axis, down)
        x = jnp.concatenate([before, x, after], axis=dim)
    return x


def find_mirror(pair_list):
    first_orb = pair_list[:, 0]
    second = pair_list[:, 1]
    matches = (first_orb[:, None] == second[None, :]) & (second[:, None] == first_orb[None, :])
    columns = jnp.arange(pair_list.shape[0], dtype=jnp.int32)
    return jnp.sum(jnp.where(matches, columns[None, :], 0), axis=1)


def to_grid(totals, a_tiles, b_tiles):
    pair_count = totals.shape[1]
    shaped = totals.reshape(a_tiles, b_tiles, pair_count, ATS, TS)
    return jnp.transpose(shaped, (2, 0, 3, 1, 4)).reshape(pair_count, a_tiles * ATS, b_tiles * TS)


def slot_kernel(picked_ref, ab_ref, live_ref, before_ref, own_ref, after_ref,
                block_ref, out_ref, amp_ref, acc_ref):
    step = pl.program_id(0)
    shard_tiles = own_ref.shape[0]

    @pl.when(step == 0)
    def _():
        acc_ref[...] = jnp.zeros_like(acc_ref)
        for side, source in enumerate((before_ref, own_ref, after_ref)):
            amp_ref[side * shard_tiles:(side + 1) * shard_tiles] = source[...]

    @pl.when(step * GROUP < live_ref[0])
    def _():
        for j in range(GROUP):
            slot = step * GROUP + j
            product = lax.dot_general(
                amp_ref[picked_ref[slot]],
                block_ref[j],
                (((1,), (1,)), ((), ())),
                precision=lax.Precision.HIGH,
                preferred_element_type=jnp.float32,
            )
            target = ab_ref[slot]
            used = slot < live_ref[0]
            acc_ref[target] = acc_ref[target] + jnp.where(used, product, 0.0)

    @pl.when(step == pl.num_programs(0) - 1)
    def _():
        out_ref[...] = acc_ref[...]


def slot_products(picked, ab_local, live, before, own, after, blocks, tiles_ab):
    slots, block_width, width = blocks.shape
    pairs = own.shape[1]
    steps = slots // GROUP

    def block_map(i, *refs):
        last = jnp.maximum(refs[2][0] - 1, 0) // GROUP
        return (jnp.minimum(i, last), 0, 0)

    whole = lambda shape: pl.BlockSpec(shape, lambda i, *_: (0,) * len(shape))
    out_shape = (tiles_ab, pairs, block_width)
    grid_spec = pltpu.PrefetchScalarGridSpec(
        num_scalar_prefetch=3,
        grid=(steps,),
        in_specs=[
            whole(before.shape),
            whole(own.shape),
            whole(after.shape),
            pl.BlockSpec((GROUP, block_width, width), block_map),
        ],
        out_specs=whole(out_shape),
        scratch_shapes=[
            pltpu.VMEM((3 * own.shape[0],) + own.shape[1:], jnp.float32),
            pltpu.VMEM((tiles_ab, pairs, block_width), jnp.float32),
        ],
    )
    return pl.pallas_call(
        slot_kernel,
        grid_spec=grid_spec,
        out_shape=jax.ShapeDtypeStruct(out_shape, jnp.float32),
        compiler_params=pltpu.CompilerParams(
            dimension_semantics=("arbitrary",), vmem_limit_bytes=48 * 1024 * 1024
        ),
        cost_estimate=pl.CostEstimate(
            flops=2 * slots * pairs * width * block_width * 3,
            bytes_accessed=4 * (slots * block_width * width + 3 * own.size + tiles_ab * pairs * block_width),
            transcendentals=0,
        ),
    )(picked, ab_local, live, before, own, after, blocks)


def exchange_rows(mirrored):
    size = lax.axis_size("row")
    index = lax.axis_index("row")
    width = mirrored.shape[1]
    placed = jnp.zeros((1, size * width, width), mirrored.dtype)
    for shift in range(size):
        block = lax.dynamic_slice_in_dim(mirrored, ((index + shift) % size) * width, width, axis=2)
        if shift:
            block = lax.ppermute(block, "row", [(i, (i + shift) % size) for i in range(size)])
        source = (index - shift + size) % size
        placed = lax.dynamic_update_slice_in_dim(placed, block, source * width, axis=1)
    return placed


def shards(amplitudes, integrals, slot_ab, slot_cd, live_count, pair_list):
    tile_size = lax.axis_size(TILE)
    row_size = lax.axis_size("row")
    tile_index = lax.axis_index(TILE)
    core = lax.axis_index("c")
    cores = lax.axis_size("c")
    shard_tiles = amplitudes.shape[0]
    pair_count = amplitudes.shape[1]
    up = [(i, (i + 1) % tile_size) for i in range(tile_size)]
    down = [(j, i) for i, j in up]
    before = lax.ppermute(amplitudes, TILE, up)
    after = lax.ppermute(amplitudes, TILE, down)
    mirror = find_mirror(pair_list)
    chips_of = jnp.arange(pair_count // cores, dtype=jnp.int32) * cores
    kept = chips_of + core
    sent = chips_of + (cores - 1 - core)
    keep_rows = jnp.concatenate([kept, mirror[kept]])
    send_rows = jnp.concatenate([sent, mirror[sent]])
    cd_global = slot_cd[0]
    owner_tile = cd_global // shard_tiles
    offset = (owner_tile - tile_index + 1 + tile_size) % tile_size
    a_tiles = SLAB // (row_size * ATS)
    b_tiles = SLAB // TS
    tiles_ab = a_tiles * b_tiles
    totals = slot_products(
        (offset * shard_tiles + cd_global % shard_tiles).astype(jnp.int32),
        slot_ab[0],
        live_count[0],
        before,
        amplitudes,
        after,
        integrals[0],
        tiles_ab,
    )
    mine = jnp.take(totals, keep_rows, axis=1)
    other = jnp.take(totals, send_rows, axis=1)
    summed = mine + lax.ppermute(other, "c", [(0, 1), (1, 0)])
    halves = summed.reshape(tiles_ab, 2, pair_count // cores, summed.shape[2])
    spread = lax.all_to_all(halves, CHIPS, 2, 2, tiled=True)
    reduced = jnp.sum(spread, axis=2)
    own = to_grid(reduced[:, 0][:, None], a_tiles, b_tiles)
    mirrored = to_grid(reduced[:, 1][:, None], a_tiles, b_tiles)
    turned = jnp.transpose(exchange_rows(mirrored), (0, 2, 1))
    return own + turned


def solution(mesh):
    tile_size = mesh.shape["tile"]
    row_size = mesh.shape["row"]
    cores = 2
    split = Mesh(
        mesh.devices.reshape(4, tile_size // (4 * cores), cores, row_size), ("x", "z", "c", "row")
    )
    return jax.shard_map(
        shards,
        mesh=split,
        in_specs=(
            P(TILE, None, None),
            P("row", TILE, None, None),
            P("row", TILE),
            P("row", TILE),
            P("row", TILE),
            P(),
        ),
        out_specs=P(TILE, "row", None),
        check_vma=False,
    )
```

```python
import functools

import jax
import jax.numpy as jnp
from jax import lax
from jax.experimental import pallas as pl
from jax.experimental.pallas import tpu as pltpu
from jax.sharding import Mesh, PartitionSpec as P

TS = 16
ATS = 8
SLAB = 96
GROUP = 16
CHIPS = ("x", "z")
TILE = ("x", "z", "c")


def padded(x, sides, width):
    for axis, dim in sides:
        size, length = (lax.axis_size(axis), x.shape[dim])
        up = [(i, (i + 1) % size) for i in range(size)]
        down = [(j, i) for i, j in up]
        last = lax.slice_in_dim(x, length - width, length, axis=dim)
        first = lax.slice_in_dim(x, 0, width, axis=dim)
        before = lax.ppermute(last, axis, up)
        after = lax.ppermute(first, axis, down)
        x = jnp.concatenate([before, x, after], axis=dim)
    return x


def find_mirror(pair_list):
    first_orb = pair_list[:, 0]
    second = pair_list[:, 1]
    matches = (first_orb[:, None] == second[None, :]) & (second[:, None] == first_orb[None, :])
    columns = jnp.arange(pair_list.shape[0], dtype=jnp.int32)
    return jnp.sum(jnp.where(matches, columns[None, :], 0), axis=1)


def to_grid(totals, a_tiles, b_tiles):
    pair_count = totals.shape[1]
    shaped = totals.reshape(a_tiles, b_tiles, pair_count, ATS, TS)
    return jnp.transpose(shaped, (2, 0, 3, 1, 4)).reshape(pair_count, a_tiles * ATS, b_tiles * TS)


def slot_kernel(index_ref, live_ref, before_ref, own_ref, after_ref,
                block_ref, out_ref, amp_ref, acc_ref, sem_ref):
    step = pl.program_id(0)
    shard_tiles = own_ref.shape[0]
    slots = index_ref.shape[0] // 2

    @pl.when(step == 0)
    def _():
        fetch = pltpu.make_async_copy(
            own_ref, amp_ref.at[shard_tiles:2 * shard_tiles], sem_ref.at[0]
        )
        fetch.start()
        acc_ref[...] = jnp.zeros_like(acc_ref)
        amp_ref[:shard_tiles] = before_ref[...]
        amp_ref[2 * shard_tiles:] = after_ref[...]
        fetch.wait()

    @pl.when(step * GROUP < live_ref[0])
    def _():
        for j in range(GROUP):
            slot = step * GROUP + j
            product = lax.dot_general(
                amp_ref[index_ref[slot]],
                block_ref[j],
                (((1,), (1,)), ((), ())),
                precision=lax.Precision.HIGH,
                preferred_element_type=jnp.float32,
            )
            target = index_ref[slots + slot]
            used = slot < live_ref[0]
            acc_ref[target] = acc_ref[target] + jnp.where(used, product, 0.0)

    @pl.when(step == pl.num_programs(0) - 1)
    def _():
        out_ref[...] = acc_ref[...]


def slot_products(index, live, before, own, after, blocks, tiles_ab):
    slots, block_width, width = blocks.shape
    pairs = own.shape[1]
    steps = slots // GROUP

    def block_map(i, *refs):
        last = jnp.maximum(refs[1][0] - 1, 0) // GROUP
        return (jnp.minimum(i, last), 0, 0)

    whole = lambda shape: pl.BlockSpec(shape, lambda i, *_: (0,) * len(shape))
    out_shape = (tiles_ab, pairs, block_width)
    grid_spec = pltpu.PrefetchScalarGridSpec(
        num_scalar_prefetch=2,
        grid=(steps,),
        in_specs=[
            whole(before.shape),
            pl.BlockSpec(memory_space=pltpu.HBM),
            whole(after.shape),
            pl.BlockSpec((GROUP, block_width, width), block_map),
        ],
        out_specs=whole(out_shape),
        scratch_shapes=[
            pltpu.VMEM((3 * own.shape[0],) + own.shape[1:], jnp.float32),
            pltpu.VMEM((tiles_ab, pairs, block_width), jnp.float32),
            pltpu.SemaphoreType.DMA((1,)),
        ],
    )
    return pl.pallas_call(
        slot_kernel,
        grid_spec=grid_spec,
        out_shape=jax.ShapeDtypeStruct(out_shape, jnp.float32),
        compiler_params=pltpu.CompilerParams(
            dimension_semantics=("arbitrary",), vmem_limit_bytes=48 * 1024 * 1024
        ),
        cost_estimate=pl.CostEstimate(
            flops=2 * slots * pairs * width * block_width * 3,
            bytes_accessed=4 * (slots * block_width * width + 3 * own.size + tiles_ab * pairs * block_width),
            transcendentals=0,
        ),
    )(index, live, before, own, after, blocks)


def exchange_rows(mirrored):
    size = lax.axis_size("row")
    index = lax.axis_index("row")
    width = mirrored.shape[1]
    placed = jnp.zeros((1, size * width, width), mirrored.dtype)
    for shift in range(size):
        block = lax.dynamic_slice_in_dim(mirrored, ((index + shift) % size) * width, width, axis=2)
        if shift:
            block = lax.ppermute(block, "row", [(i, (i + shift) % size) for i in range(size)])
        source = (index - shift + size) % size
        placed = lax.dynamic_update_slice_in_dim(placed, block, source * width, axis=1)
    return placed


def shards(amplitudes, integrals, slot_ab, slot_cd, live_count, pair_list):
    tile_size = lax.axis_size(TILE)
    row_size = lax.axis_size("row")
    tile_index = lax.axis_index(TILE)
    core = lax.axis_index("c")
    cores = lax.axis_size("c")
    shard_tiles = amplitudes.shape[0]
    pair_count = amplitudes.shape[1]
    up = [(i, (i + 1) % tile_size) for i in range(tile_size)]
    down = [(j, i) for i, j in up]
    before = lax.ppermute(amplitudes, TILE, up)
    after = lax.ppermute(amplitudes, TILE, down)
    mirror = find_mirror(pair_list)
    chips_of = jnp.arange(pair_count // cores, dtype=jnp.int32) * cores
    kept = chips_of + core
    sent = chips_of + (cores - 1 - core)
    keep_rows = jnp.concatenate([kept, mirror[kept]])
    send_rows = jnp.concatenate([sent, mirror[sent]])
    cd_global = slot_cd[0]
    owner_tile = cd_global // shard_tiles
    offset = (owner_tile - tile_index + 1 + tile_size) % tile_size
    a_tiles = SLAB // (row_size * ATS)
    b_tiles = SLAB // TS
    tiles_ab = a_tiles * b_tiles
    totals = slot_products(
        jnp.concatenate([offset * shard_tiles + cd_global % shard_tiles, slot_ab[0]]).astype(jnp.int32),
        live_count[0],
        before,
        amplitudes,
        after,
        integrals[0],
        tiles_ab,
    )
    mine = jnp.take(totals, keep_rows, axis=1)
    other = jnp.take(totals, send_rows, axis=1)
    summed = mine + lax.ppermute(other, "c", [(0, 1), (1, 0)])
    halves = summed.reshape(tiles_ab, 2, pair_count // cores, summed.shape[2])
    spread = lax.all_to_all(halves, CHIPS, 2, 2, tiled=True)
    reduced = jnp.sum(spread, axis=2)
    own = to_grid(reduced[:, 0][:, None], a_tiles, b_tiles)
    mirrored = to_grid(reduced[:, 1][:, None], a_tiles, b_tiles)
    turned = jnp.transpose(exchange_rows(mirrored), (0, 2, 1))
    return own + turned


def solution(mesh):
    tile_size = mesh.shape["tile"]
    row_size = mesh.shape["row"]
    cores = 2
    split = Mesh(
        mesh.devices.reshape(4, tile_size // (4 * cores), cores, row_size), ("x", "z", "c", "row")
    )
    return jax.shard_map(
        shards,
        mesh=split,
        in_specs=(
            P(TILE, None, None),
            P("row", TILE, None, None),
            P("row", TILE),
            P("row", TILE),
            P("row", TILE),
            P(),
        ),
        out_specs=P(TILE, "row", None),
        check_vma=False,
    )
```

```python
import functools

import jax
import jax.numpy as jnp
from jax import lax
from jax.experimental import pallas as pl
from jax.experimental.pallas import tpu as pltpu
from jax.sharding import Mesh, PartitionSpec as P

TS = 16
ATS = 8
SLAB = 96
GROUP = 16
CHIPS = ("x", "z")
TILE = ("x", "z", "c")


def padded(x, sides, width):
    for axis, dim in sides:
        size, length = (lax.axis_size(axis), x.shape[dim])
        up = [(i, (i + 1) % size) for i in range(size)]
        down = [(j, i) for i, j in up]
        last = lax.slice_in_dim(x, length - width, length, axis=dim)
        first = lax.slice_in_dim(x, 0, width, axis=dim)
        before = lax.ppermute(last, axis, up)
        after = lax.ppermute(first, axis, down)
        x = jnp.concatenate([before, x, after], axis=dim)
    return x


def find_mirror(pair_list):
    first_orb = pair_list[:, 0]
    second = pair_list[:, 1]
    matches = (first_orb[:, None] == second[None, :]) & (second[:, None] == first_orb[None, :])
    columns = jnp.arange(pair_list.shape[0], dtype=jnp.int32)
    return jnp.sum(jnp.where(matches, columns[None, :], 0), axis=1)


def to_grid(totals, a_tiles, b_tiles):
    pair_count = totals.shape[1]
    shaped = totals.reshape(a_tiles, b_tiles, pair_count, ATS, TS)
    return jnp.transpose(shaped, (2, 0, 3, 1, 4)).reshape(pair_count, a_tiles * ATS, b_tiles * TS)


def slot_kernel(index_ref, live_ref, before_ref, own_ref, after_ref,
                block_ref, out_ref, amp_ref, acc_ref, sem_ref):
    step = pl.program_id(0)
    shard_tiles = own_ref.shape[0]
    slots = index_ref.shape[0] // 2

    @pl.when(step == 0)
    def _():
        fetch = pltpu.make_async_copy(
            own_ref, amp_ref.at[shard_tiles:2 * shard_tiles], sem_ref.at[0]
        )
        fetch.start()
        acc_ref[...] = jnp.zeros_like(acc_ref)
        amp_ref[:shard_tiles] = before_ref[...]
        amp_ref[2 * shard_tiles:] = after_ref[...]
        fetch.wait()

    @pl.when(step * GROUP < live_ref[0])
    def _():
        for j in range(GROUP):
            slot = step * GROUP + j
            product = lax.dot_general(
                amp_ref[index_ref[slot]],
                block_ref[j],
                (((1,), (1,)), ((), ())),
                precision=lax.Precision.HIGHEST,
                preferred_element_type=jnp.float32,
            )
            target = index_ref[slots + slot]
            used = slot < live_ref[0]
            acc_ref[target] = acc_ref[target] + jnp.where(used, product, 0.0)

    @pl.when(step == pl.num_programs(0) - 1)
    def _():
        out_ref[...] = acc_ref[...]


def slot_products(index, live, before, own, after, blocks, tiles_ab):
    slots, block_width, width = blocks.shape
    pairs = own.shape[1]
    steps = slots // GROUP

    def block_map(i, *refs):
        last = jnp.maximum(refs[1][0] - 1, 0) // GROUP
        return (jnp.minimum(i, last), 0, 0)

    whole = lambda shape: pl.BlockSpec(shape, lambda i, *_: (0,) * len(shape))
    out_shape = (tiles_ab, pairs, block_width)
    grid_spec = pltpu.PrefetchScalarGridSpec(
        num_scalar_prefetch=2,
        grid=(steps,),
        in_specs=[
            whole(before.shape),
            pl.BlockSpec(memory_space=pltpu.HBM),
            whole(after.shape),
            pl.BlockSpec((GROUP, block_width, width), block_map),
        ],
        out_specs=whole(out_shape),
        scratch_shapes=[
            pltpu.VMEM((3 * own.shape[0],) + own.shape[1:], jnp.float32),
            pltpu.VMEM((tiles_ab, pairs, block_width), jnp.float32),
            pltpu.SemaphoreType.DMA((1,)),
        ],
    )
    return pl.pallas_call(
        slot_kernel,
        grid_spec=grid_spec,
        out_shape=jax.ShapeDtypeStruct(out_shape, jnp.float32),
        compiler_params=pltpu.CompilerParams(
            dimension_semantics=("arbitrary",), vmem_limit_bytes=48 * 1024 * 1024
        ),
        cost_estimate=pl.CostEstimate(
            flops=2 * slots * pairs * width * block_width * 6,
            bytes_accessed=4 * (slots * block_width * width + 3 * own.size + tiles_ab * pairs * block_width),
            transcendentals=0,
        ),
    )(index, live, before, own, after, blocks)


def exchange_rows(mirrored):
    size = lax.axis_size("row")
    index = lax.axis_index("row")
    width = mirrored.shape[1]
    placed = jnp.zeros((1, size * width, width), mirrored.dtype)
    for shift in range(size):
        block = lax.dynamic_slice_in_dim(mirrored, ((index + shift) % size) * width, width, axis=2)
        if shift:
            block = lax.ppermute(block, "row", [(i, (i + shift) % size) for i in range(size)])
        source = (index - shift + size) % size
        placed = lax.dynamic_update_slice_in_dim(placed, block, source * width, axis=1)
    return placed


def shards(amplitudes, integrals, slot_ab, slot_cd, live_count, pair_list):
    tile_size = lax.axis_size(TILE)
    row_size = lax.axis_size("row")
    tile_index = lax.axis_index(TILE)
    core = lax.axis_index("c")
    cores = lax.axis_size("c")
    shard_tiles = amplitudes.shape[0]
    pair_count = amplitudes.shape[1]
    up = [(i, (i + 1) % tile_size) for i in range(tile_size)]
    down = [(j, i) for i, j in up]
    before = lax.ppermute(amplitudes, TILE, up)
    after = lax.ppermute(amplitudes, TILE, down)
    mirror = find_mirror(pair_list)
    chips_of = jnp.arange(pair_count // cores, dtype=jnp.int32) * cores
    kept = chips_of + core
    sent = chips_of + (cores - 1 - core)
    keep_rows = jnp.concatenate([kept, mirror[kept]])
    send_rows = jnp.concatenate([sent, mirror[sent]])
    cd_global = slot_cd[0]
    owner_tile = cd_global // shard_tiles
    offset = (owner_tile - tile_index + 1 + tile_size) % tile_size
    a_tiles = SLAB // (row_size * ATS)
    b_tiles = SLAB // TS
    tiles_ab = a_tiles * b_tiles
    totals = slot_products(
        jnp.concatenate([offset * shard_tiles + cd_global % shard_tiles, slot_ab[0]]).astype(jnp.int32),
        live_count[0],
        before,
        amplitudes,
        after,
        integrals[0],
        tiles_ab,
    )
    mine = jnp.take(totals, keep_rows, axis=1)
    other = jnp.take(totals, send_rows, axis=1)
    summed = mine + lax.ppermute(other, "c", [(0, 1), (1, 0)])
    halves = summed.reshape(tiles_ab, 2, pair_count // cores, summed.shape[2])
    spread = lax.all_to_all(halves, CHIPS, 2, 2, tiled=True)
    reduced = jnp.sum(spread, axis=2)
    own = to_grid(reduced[:, 0][:, None], a_tiles, b_tiles)
    mirrored = to_grid(reduced[:, 1][:, None], a_tiles, b_tiles)
    turned = jnp.transpose(exchange_rows(mirrored), (0, 2, 1))
    return own + turned


def solution(mesh):
    tile_size = mesh.shape["tile"]
    row_size = mesh.shape["row"]
    cores = 2
    split = Mesh(
        mesh.devices.reshape(4, tile_size // (4 * cores), cores, row_size), ("x", "z", "c", "row")
    )
    return jax.shard_map(
        shards,
        mesh=split,
        in_specs=(
            P(TILE, None, None),
            P("row", TILE, None, None),
            P("row", TILE),
            P("row", TILE),
            P("row", TILE),
            P(),
        ),
        out_specs=P(TILE, "row", None),
        check_vma=False,
    )
```

```python
import functools

import jax
import jax.numpy as jnp
from jax import lax
from jax.experimental import pallas as pl
from jax.experimental.pallas import tpu as pltpu
from jax.sharding import Mesh, PartitionSpec as P

TS = 16
ATS = 8
SLAB = 96
GROUP = 16
CHIPS = ("x", "z")
TILE = ("x", "z", "c")


def padded(x, sides, width):
    for axis, dim in sides:
        size, length = (lax.axis_size(axis), x.shape[dim])
        up = [(i, (i + 1) % size) for i in range(size)]
        down = [(j, i) for i, j in up]
        last = lax.slice_in_dim(x, length - width, length, axis=dim)
        first = lax.slice_in_dim(x, 0, width, axis=dim)
        before = lax.ppermute(last, axis, up)
        after = lax.ppermute(first, axis, down)
        x = jnp.concatenate([before, x, after], axis=dim)
    return x


def find_mirror(pair_list):
    first_orb = pair_list[:, 0]
    second = pair_list[:, 1]
    matches = (first_orb[:, None] == second[None, :]) & (second[:, None] == first_orb[None, :])
    columns = jnp.arange(pair_list.shape[0], dtype=jnp.int32)
    return jnp.sum(jnp.where(matches, columns[None, :], 0), axis=1)


def to_grid(totals, a_tiles, b_tiles):
    pair_count = totals.shape[1]
    shaped = totals.reshape(a_tiles, b_tiles, pair_count, ATS, TS)
    return jnp.transpose(shaped, (2, 0, 3, 1, 4)).reshape(pair_count, a_tiles * ATS, b_tiles * TS)


def slot_kernel(index_ref, live_ref, before_ref, own_ref, after_ref,
                block_ref, out_ref, amp_ref, acc_ref, sem_ref):
    step = pl.program_id(0)
    shard_tiles = own_ref.shape[0]
    slots = index_ref.shape[0] // 2

    @pl.when(step == 0)
    def _():
        fetch = pltpu.make_async_copy(
            own_ref, amp_ref.at[shard_tiles:2 * shard_tiles], sem_ref.at[0]
        )
        fetch.start()
        acc_ref[...] = jnp.zeros_like(acc_ref)
        amp_ref[:shard_tiles] = before_ref[...]
        amp_ref[2 * shard_tiles:] = after_ref[...]
        fetch.wait()

    @pl.when(step * GROUP < live_ref[0])
    def _():
        for j in range(GROUP):
            slot = step * GROUP + j
            product = lax.dot_general(
                amp_ref[index_ref[slot]],
                block_ref[j],
                (((1,), (1,)), ((), ())),
                precision=lax.Precision.HIGHEST,
                preferred_element_type=jnp.float32,
            )
            target = index_ref[slots + slot]
            used = slot < live_ref[0]
            acc_ref[target] = acc_ref[target] + jnp.where(used, product, 0.0)

    @pl.when(step == pl.num_programs(0) - 1)
    def _():
        out_ref[...] = acc_ref[...]


def slot_products(index, live, before, own, after, blocks, tiles_ab):
    slots, block_width, width = blocks.shape
    pairs = own.shape[1]
    steps = slots // GROUP

    def block_map(i, *refs):
        last = jnp.maximum(refs[1][0] - 1, 0) // GROUP
        return (jnp.minimum(i, last), 0, 0)

    whole = lambda shape: pl.BlockSpec(shape, lambda i, *_: (0,) * len(shape))
    out_shape = (tiles_ab, pairs, block_width)
    grid_spec = pltpu.PrefetchScalarGridSpec(
        num_scalar_prefetch=2,
        grid=(steps,),
        in_specs=[
            whole(before.shape),
            pl.BlockSpec(memory_space=pltpu.HBM),
            whole(after.shape),
            pl.BlockSpec((GROUP, block_width, width), block_map),
        ],
        out_specs=whole(out_shape),
        scratch_shapes=[
            pltpu.VMEM((3 * own.shape[0],) + own.shape[1:], jnp.float32),
            pltpu.VMEM((tiles_ab, pairs, block_width), jnp.float32),
            pltpu.SemaphoreType.DMA((1,)),
        ],
    )
    return pl.pallas_call(
        slot_kernel,
        grid_spec=grid_spec,
        out_shape=jax.ShapeDtypeStruct(out_shape, jnp.float32),
        compiler_params=pltpu.CompilerParams(
            dimension_semantics=("arbitrary",), vmem_limit_bytes=48 * 1024 * 1024
        ),
        cost_estimate=pl.CostEstimate(
            flops=2 * slots * pairs * width * block_width * 6,
            bytes_accessed=4 * (slots * block_width * width + 3 * own.size + tiles_ab * pairs * block_width),
            transcendentals=0,
        ),
    )(index, live, before, own, after, blocks)


def exchange_rows(mirrored):
    size = lax.axis_size("row")
    index = lax.axis_index("row")
    width = mirrored.shape[1]
    placed = jnp.zeros((1, size * width, width), mirrored.dtype)
    for shift in range(size):
        block = lax.dynamic_slice_in_dim(mirrored, ((index + shift) % size) * width, width, axis=2)
        if shift:
            block = lax.ppermute(block, "row", [(i, (i + shift) % size) for i in range(size)])
        source = (index - shift + size) % size
        placed = lax.dynamic_update_slice_in_dim(placed, block, source * width, axis=1)
    return placed


def shards(amplitudes, integrals, slot_ab, slot_cd, live_count, pair_list):
    tile_size = lax.axis_size(TILE)
    row_size = lax.axis_size("row")
    tile_index = lax.axis_index(TILE)
    core = lax.axis_index("c")
    cores = lax.axis_size("c")
    shard_tiles = amplitudes.shape[0]
    pair_count = amplitudes.shape[1]
    up = [(i, (i + 1) % tile_size) for i in range(tile_size)]
    down = [(j, i) for i, j in up]
    before = lax.ppermute(amplitudes, TILE, up)
    after = lax.ppermute(amplitudes, TILE, down)
    mirror = find_mirror(pair_list)
    chips_of = jnp.arange(pair_count // cores, dtype=jnp.int32) * cores
    kept = chips_of + core
    sent = chips_of + (cores - 1 - core)
    keep_rows = jnp.concatenate([kept, mirror[kept]])
    send_rows = jnp.concatenate([sent, mirror[sent]])
    cd_global = slot_cd[0]
    owner_tile = cd_global // shard_tiles
    offset = (owner_tile - tile_index + 1 + tile_size) % tile_size
    a_tiles = SLAB // (row_size * ATS)
    b_tiles = SLAB // TS
    tiles_ab = a_tiles * b_tiles
    totals = slot_products(
        jnp.concatenate([offset * shard_tiles + cd_global % shard_tiles, slot_ab[0]]).astype(jnp.int32),
        live_count[0],
        before,
        amplitudes,
        after,
        integrals[0],
        tiles_ab,
    )
    pairs_axis = jnp.arange(pair_count, dtype=jnp.int32)[None, :]
    pick = lambda rows: jnp.einsum(
        "qp,epb->eqb",
        (rows[:, None] == pairs_axis).astype(jnp.float32),
        totals,
        precision=lax.Precision.HIGHEST,
        preferred_element_type=jnp.float32,
    )
    mine = pick(keep_rows)
    other = pick(send_rows)
    summed = mine + lax.ppermute(other, "c", [(0, 1), (1, 0)])
    halves = summed.reshape(tiles_ab, 2, pair_count // cores, summed.shape[2])
    spread = lax.all_to_all(halves, CHIPS, 2, 2, tiled=True)
    reduced = jnp.sum(spread, axis=2)
    own = to_grid(reduced[:, 0][:, None], a_tiles, b_tiles)
    mirrored = to_grid(reduced[:, 1][:, None], a_tiles, b_tiles)
    turned = jnp.transpose(exchange_rows(mirrored), (0, 2, 1))
    return own + turned


def solution(mesh):
    tile_size = mesh.shape["tile"]
    row_size = mesh.shape["row"]
    cores = 2
    split = Mesh(
        mesh.devices.reshape(4, tile_size // (4 * cores), cores, row_size), ("x", "z", "c", "row")
    )
    return jax.shard_map(
        shards,
        mesh=split,
        in_specs=(
            P(TILE, None, None),
            P("row", TILE, None, None),
            P("row", TILE),
            P("row", TILE),
            P("row", TILE),
            P(),
        ),
        out_specs=P(TILE, "row", None),
        check_vma=False,
    )
```

```python
import functools

import jax
import jax.numpy as jnp
from jax import lax
from jax.experimental import pallas as pl
from jax.experimental.pallas import tpu as pltpu
from jax.sharding import Mesh, PartitionSpec as P

TS = 16
ATS = 8
SLAB = 96
GROUP = 16
CHIPS = ("x", "z")
TILE = ("x", "z", "c")


def padded(x, sides, width):
    for axis, dim in sides:
        size, length = (lax.axis_size(axis), x.shape[dim])
        up = [(i, (i + 1) % size) for i in range(size)]
        down = [(j, i) for i, j in up]
        last = lax.slice_in_dim(x, length - width, length, axis=dim)
        first = lax.slice_in_dim(x, 0, width, axis=dim)
        before = lax.ppermute(last, axis, up)
        after = lax.ppermute(first, axis, down)
        x = jnp.concatenate([before, x, after], axis=dim)
    return x


def find_mirror(pair_list):
    first_orb = pair_list[:, 0]
    second = pair_list[:, 1]
    matches = (first_orb[:, None] == second[None, :]) & (second[:, None] == first_orb[None, :])
    columns = jnp.arange(pair_list.shape[0], dtype=jnp.int32)
    return jnp.sum(jnp.where(matches, columns[None, :], 0), axis=1)


def to_grid(totals, a_tiles, b_tiles):
    pair_count = totals.shape[1]
    shaped = totals.reshape(a_tiles, b_tiles, pair_count, ATS, TS)
    return jnp.transpose(shaped, (2, 0, 3, 1, 4)).reshape(pair_count, a_tiles * ATS, b_tiles * TS)


def slot_kernel(index_ref, live_ref, before_ref, own_ref, after_ref,
                block_ref, out_ref, amp_ref, acc_ref, sem_ref):
    step = pl.program_id(0)
    shard_tiles = own_ref.shape[0]
    slots = index_ref.shape[0] // 2

    @pl.when(step == 0)
    def _():
        fetch = pltpu.make_async_copy(
            own_ref, amp_ref.at[shard_tiles:2 * shard_tiles], sem_ref.at[0]
        )
        fetch.start()
        acc_ref[...] = jnp.zeros_like(acc_ref)
        amp_ref[:shard_tiles] = before_ref[...]
        amp_ref[2 * shard_tiles:] = after_ref[...]
        fetch.wait()

    @pl.when(step * GROUP < live_ref[0])
    def _():
        for j in range(GROUP):
            slot = step * GROUP + j
            product = lax.dot_general(
                amp_ref[index_ref[slot]],
                block_ref[j],
                (((1,), (1,)), ((), ())),
                precision=lax.Precision.HIGHEST,
                preferred_element_type=jnp.float32,
            )
            target = index_ref[slots + slot]
            used = slot < live_ref[0]
            acc_ref[target] = acc_ref[target] + jnp.where(used, product, 0.0)

    @pl.when(step == pl.num_programs(0) - 1)
    def _():
        out_ref[...] = acc_ref[...]


def slot_products(index, live, before, own, after, blocks, tiles_ab):
    slots, block_width, width = blocks.shape
    pairs = own.shape[1]
    steps = slots // GROUP

    def block_map(i, *refs):
        last = jnp.maximum(refs[1][0] - 1, 0) // GROUP
        return (jnp.minimum(i, last), 0, 0)

    whole = lambda shape: pl.BlockSpec(shape, lambda i, *_: (0,) * len(shape))
    out_shape = (tiles_ab, pairs, block_width)
    grid_spec = pltpu.PrefetchScalarGridSpec(
        num_scalar_prefetch=2,
        grid=(steps,),
        in_specs=[
            whole(before.shape),
            pl.BlockSpec(memory_space=pltpu.HBM),
            whole(after.shape),
            pl.BlockSpec((GROUP, block_width, width), block_map),
        ],
        out_specs=whole(out_shape),
        scratch_shapes=[
            pltpu.VMEM((3 * own.shape[0],) + own.shape[1:], jnp.float32),
            pltpu.VMEM((tiles_ab, pairs, block_width), jnp.float32),
            pltpu.SemaphoreType.DMA((1,)),
        ],
    )
    return pl.pallas_call(
        slot_kernel,
        grid_spec=grid_spec,
        out_shape=jax.ShapeDtypeStruct(out_shape, jnp.float32),
        compiler_params=pltpu.CompilerParams(
            dimension_semantics=("arbitrary",), vmem_limit_bytes=48 * 1024 * 1024
        ),
        cost_estimate=pl.CostEstimate(
            flops=2 * slots * pairs * width * block_width * 6,
            bytes_accessed=4 * (slots * block_width * width + 3 * own.size + tiles_ab * pairs * block_width),
            transcendentals=0,
        ),
    )(index, live, before, own, after, blocks)


def exchange_rows(mirrored):
    size = lax.axis_size("row")
    index = lax.axis_index("row")
    width = mirrored.shape[1]
    placed = jnp.zeros((1, size * width, width), mirrored.dtype)
    for shift in range(size):
        block = lax.dynamic_slice_in_dim(mirrored, ((index + shift) % size) * width, width, axis=2)
        if shift:
            block = lax.ppermute(block, "row", [(i, (i + shift) % size) for i in range(size)])
        source = (index - shift + size) % size
        placed = lax.dynamic_update_slice_in_dim(placed, block, source * width, axis=1)
    return placed


def shards(amplitudes, integrals, slot_ab, slot_cd, live_count, pair_list):
    tile_size = lax.axis_size(TILE)
    row_size = lax.axis_size("row")
    tile_index = lax.axis_index(TILE)
    core = lax.axis_index("c")
    cores = lax.axis_size("c")
    shard_tiles = amplitudes.shape[0]
    pair_count = amplitudes.shape[1]
    up = [(i, (i + 1) % tile_size) for i in range(tile_size)]
    down = [(j, i) for i, j in up]
    before = lax.ppermute(amplitudes, TILE, up)
    after = lax.ppermute(amplitudes, TILE, down)
    mirror = find_mirror(pair_list)
    chips_of = jnp.arange(pair_count // cores, dtype=jnp.int32) * cores
    kept = chips_of + core
    sent = chips_of + (cores - 1 - core)
    keep_rows = jnp.concatenate([kept, mirror[kept]])
    send_rows = jnp.concatenate([sent, mirror[sent]])
    cd_global = slot_cd[0]
    owner_tile = cd_global // shard_tiles
    offset = (owner_tile - tile_index + 1 + tile_size) % tile_size
    a_tiles = SLAB // (row_size * ATS)
    b_tiles = SLAB // TS
    tiles_ab = a_tiles * b_tiles
    totals = slot_products(
        jnp.concatenate([offset * shard_tiles + cd_global % shard_tiles, slot_ab[0]]).astype(jnp.int32),
        live_count[0],
        before,
        amplitudes,
        after,
        integrals[0],
        tiles_ab,
    )
    pairs_axis = jnp.arange(pair_count, dtype=jnp.int32)[None, :]
    chips = pair_count // cores
    pick = lambda rows: jnp.einsum(
        "qp,epb->qeb",
        (rows.reshape(2, chips).T.reshape(-1)[:, None] == pairs_axis).astype(jnp.float32),
        totals,
        precision=lax.Precision.HIGHEST,
        preferred_element_type=jnp.float32,
    )
    mine = pick(keep_rows)
    other = pick(send_rows)
    summed = mine + lax.ppermute(other, "c", [(0, 1), (1, 0)])
    halves = summed.reshape(chips, 2 * summed.shape[1], summed.shape[2])
    spread = lax.all_to_all(halves, CHIPS, 0, 0, tiled=True)
    reduced = jnp.sum(spread, axis=0).reshape(2, tiles_ab, summed.shape[2])
    own = to_grid(reduced[0][:, None], a_tiles, b_tiles)
    mirrored = to_grid(reduced[1][:, None], a_tiles, b_tiles)
    turned = jnp.transpose(exchange_rows(mirrored), (0, 2, 1))
    return own + turned


def solution(mesh):
    tile_size = mesh.shape["tile"]
    row_size = mesh.shape["row"]
    cores = 2
    split = Mesh(
        mesh.devices.reshape(4, tile_size // (4 * cores), cores, row_size), ("x", "z", "c", "row")
    )
    return jax.shard_map(
        shards,
        mesh=split,
        in_specs=(
            P(TILE, None, None),
            P("row", TILE, None, None),
            P("row", TILE),
            P("row", TILE),
            P("row", TILE),
            P(),
        ),
        out_specs=P(TILE, "row", None),
        check_vma=False,
    )
```

```python
import functools

import jax
import jax.numpy as jnp
from jax import lax
from jax.experimental import pallas as pl
from jax.experimental.pallas import tpu as pltpu
from jax.sharding import Mesh, PartitionSpec as P

TS = 16
ATS = 8
SLAB = 96
GROUP = 16
CHIPS = ("x", "z")
TILE = ("x", "z", "c")


def padded(x, sides, width):
    for axis, dim in sides:
        size, length = (lax.axis_size(axis), x.shape[dim])
        up = [(i, (i + 1) % size) for i in range(size)]
        down = [(j, i) for i, j in up]
        last = lax.slice_in_dim(x, length - width, length, axis=dim)
        first = lax.slice_in_dim(x, 0, width, axis=dim)
        before = lax.ppermute(last, axis, up)
        after = lax.ppermute(first, axis, down)
        x = jnp.concatenate([before, x, after], axis=dim)
    return x


def find_mirror(pair_list):
    first_orb = pair_list[:, 0]
    second = pair_list[:, 1]
    matches = (first_orb[:, None] == second[None, :]) & (second[:, None] == first_orb[None, :])
    columns = jnp.arange(pair_list.shape[0], dtype=jnp.int32)
    return jnp.sum(jnp.where(matches, columns[None, :], 0), axis=1)


def to_grid(totals, a_tiles, b_tiles):
    pair_count = totals.shape[1]
    shaped = totals.reshape(a_tiles, b_tiles, pair_count, ATS, TS)
    return jnp.transpose(shaped, (2, 0, 3, 1, 4)).reshape(pair_count, a_tiles * ATS, b_tiles * TS)


def slot_kernel(index_ref, live_ref, before_ref, own_ref, after_ref,
                block_ref, out_ref, amp_ref, acc_ref, sem_ref):
    step = pl.program_id(0)
    shard_tiles = own_ref.shape[0]
    slots = index_ref.shape[0] // 2

    @pl.when(step == 0)
    def _():
        fetch = pltpu.make_async_copy(
            own_ref, amp_ref.at[shard_tiles:2 * shard_tiles], sem_ref.at[0]
        )
        fetch.start()
        acc_ref[...] = jnp.zeros_like(acc_ref)
        amp_ref[:shard_tiles] = before_ref[...]
        amp_ref[2 * shard_tiles:] = after_ref[...]
        fetch.wait()

    @pl.when(step * GROUP < live_ref[0])
    def _():
        for j in range(GROUP):
            slot = step * GROUP + j
            product = lax.dot_general(
                amp_ref[index_ref[slot]],
                block_ref[j],
                (((1,), (1,)), ((), ())),
                precision=lax.Precision.HIGHEST,
                preferred_element_type=jnp.float32,
            )
            target = index_ref[slots + slot]
            used = slot < live_ref[0]
            acc_ref[target] = acc_ref[target] + jnp.where(used, product, 0.0)

    @pl.when(step == pl.num_programs(0) - 1)
    def _():
        out_ref[...] = acc_ref[...]


def slot_products(index, live, before, own, after, blocks, tiles_ab):
    slots, block_width, width = blocks.shape
    pairs = own.shape[1]
    steps = slots // GROUP

    def block_map(i, *refs):
        last = jnp.maximum(refs[1][0] - 1, 0) // GROUP
        return (jnp.minimum(i, last), 0, 0)

    whole = lambda shape: pl.BlockSpec(shape, lambda i, *_: (0,) * len(shape))
    out_shape = (tiles_ab, pairs, block_width)
    grid_spec = pltpu.PrefetchScalarGridSpec(
        num_scalar_prefetch=2,
        grid=(steps,),
        in_specs=[
            whole(before.shape),
            pl.BlockSpec(memory_space=pltpu.HBM),
            whole(after.shape),
            pl.BlockSpec((GROUP, block_width, width), block_map),
        ],
        out_specs=whole(out_shape),
        scratch_shapes=[
            pltpu.VMEM((3 * own.shape[0],) + own.shape[1:], jnp.float32),
            pltpu.VMEM((tiles_ab, pairs, block_width), jnp.float32),
            pltpu.SemaphoreType.DMA((1,)),
        ],
    )
    return pl.pallas_call(
        slot_kernel,
        grid_spec=grid_spec,
        out_shape=jax.ShapeDtypeStruct(out_shape, jnp.float32),
        compiler_params=pltpu.CompilerParams(
            dimension_semantics=("arbitrary",), vmem_limit_bytes=48 * 1024 * 1024
        ),
        cost_estimate=pl.CostEstimate(
            flops=2 * slots * pairs * width * block_width * 6,
            bytes_accessed=4 * (slots * block_width * width + 3 * own.size + tiles_ab * pairs * block_width),
            transcendentals=0,
        ),
    )(index, live, before, own, after, blocks)


def exchange_rows(mirrored):
    size = lax.axis_size("row")
    index = lax.axis_index("row")
    width = mirrored.shape[1]
    received = [mirrored] + [
        lax.ppermute(mirrored, "row", [(i, (i + shift) % size) for i in range(size)])
        for shift in range(1, size)
    ]
    by_source = jnp.stack(received[::-1] + received[::-1], axis=0)
    start = (size - 1 - index) % size
    ordered = lax.dynamic_slice_in_dim(by_source, start, size, axis=0)
    columns = lax.dynamic_slice_in_dim(ordered, index * width, width, axis=3)
    return columns.reshape(1, size * width, width)


def shards(amplitudes, integrals, slot_ab, slot_cd, live_count, pair_list):
    tile_size = lax.axis_size(TILE)
    row_size = lax.axis_size("row")
    tile_index = lax.axis_index(TILE)
    core = lax.axis_index("c")
    cores = lax.axis_size("c")
    shard_tiles = amplitudes.shape[0]
    pair_count = amplitudes.shape[1]
    up = [(i, (i + 1) % tile_size) for i in range(tile_size)]
    down = [(j, i) for i, j in up]
    before = lax.ppermute(amplitudes, TILE, up)
    after = lax.ppermute(amplitudes, TILE, down)
    mirror = find_mirror(pair_list)
    chips_of = jnp.arange(pair_count // cores, dtype=jnp.int32) * cores
    kept = chips_of + core
    sent = chips_of + (cores - 1 - core)
    keep_rows = jnp.concatenate([kept, mirror[kept]])
    send_rows = jnp.concatenate([sent, mirror[sent]])
    cd_global = slot_cd[0]
    owner_tile = cd_global // shard_tiles
    offset = (owner_tile - tile_index + 1 + tile_size) % tile_size
    a_tiles = SLAB // (row_size * ATS)
    b_tiles = SLAB // TS
    tiles_ab = a_tiles * b_tiles
    totals = slot_products(
        jnp.concatenate([offset * shard_tiles + cd_global % shard_tiles, slot_ab[0]]).astype(jnp.int32),
        live_count[0],
        before,
        amplitudes,
        after,
        integrals[0],
        tiles_ab,
    )
    pairs_axis = jnp.arange(pair_count, dtype=jnp.int32)[None, :]
    pick = lambda rows: jnp.einsum(
        "qp,epb->eqb",
        (rows[:, None] == pairs_axis).astype(jnp.float32),
        totals,
        precision=lax.Precision.HIGHEST,
        preferred_element_type=jnp.float32,
    )
    mine = pick(keep_rows)
    other = pick(send_rows)
    summed = mine + lax.ppermute(other, "c", [(0, 1), (1, 0)])
    halves = summed.reshape(tiles_ab, 2, pair_count // cores, summed.shape[2])
    spread = lax.all_to_all(halves, CHIPS, 2, 2, tiled=True)
    reduced = jnp.sum(spread, axis=2)
    own = to_grid(reduced[:, 0][:, None], a_tiles, b_tiles)
    mirrored = to_grid(reduced[:, 1][:, None], a_tiles, b_tiles)
    turned = jnp.transpose(exchange_rows(mirrored), (0, 2, 1))
    return own + turned


def solution(mesh):
    tile_size = mesh.shape["tile"]
    row_size = mesh.shape["row"]
    cores = 2
    split = Mesh(
        mesh.devices.reshape(4, tile_size // (4 * cores), cores, row_size), ("x", "z", "c", "row")
    )
    return jax.shard_map(
        shards,
        mesh=split,
        in_specs=(
            P(TILE, None, None),
            P("row", TILE, None, None),
            P("row", TILE),
            P("row", TILE),
            P("row", TILE),
            P(),
        ),
        out_specs=P(TILE, "row", None),
        check_vma=False,
    )
```

```python
import functools

import jax
import jax.numpy as jnp
from jax import lax
from jax.experimental import pallas as pl
from jax.experimental.pallas import tpu as pltpu
from jax.sharding import Mesh, PartitionSpec as P

TS = 16
ATS = 8
SLAB = 96
GROUP = 16
CHIPS = ("x", "z")
TILE = ("x", "z", "c")


def padded(x, sides, width):
    for axis, dim in sides:
        size, length = (lax.axis_size(axis), x.shape[dim])
        up = [(i, (i + 1) % size) for i in range(size)]
        down = [(j, i) for i, j in up]
        last = lax.slice_in_dim(x, length - width, length, axis=dim)
        first = lax.slice_in_dim(x, 0, width, axis=dim)
        before = lax.ppermute(last, axis, up)
        after = lax.ppermute(first, axis, down)
        x = jnp.concatenate([before, x, after], axis=dim)
    return x


def find_mirror(pair_list):
    first_orb = pair_list[:, 0]
    second = pair_list[:, 1]
    matches = (first_orb[:, None] == second[None, :]) & (second[:, None] == first_orb[None, :])
    columns = jnp.arange(pair_list.shape[0], dtype=jnp.int32)
    return jnp.sum(jnp.where(matches, columns[None, :], 0), axis=1)


def to_grid(totals, a_tiles, b_tiles):
    pair_count = totals.shape[1]
    shaped = totals.reshape(a_tiles, b_tiles, pair_count, ATS, TS)
    return jnp.transpose(shaped, (2, 0, 3, 1, 4)).reshape(pair_count, a_tiles * ATS, b_tiles * TS)


def slot_kernel(index_ref, live_ref, before_ref, own_ref, after_ref,
                block_ref, out_ref, amp_ref, acc_ref, sem_ref):
    step = pl.program_id(0)
    shard_tiles = own_ref.shape[0]
    slots = index_ref.shape[0] // 2

    @pl.when(step == 0)
    def _():
        fetch = pltpu.make_async_copy(
            own_ref, amp_ref.at[shard_tiles:2 * shard_tiles], sem_ref.at[0]
        )
        fetch.start()
        acc_ref[...] = jnp.zeros_like(acc_ref)
        amp_ref[:shard_tiles] = before_ref[...]
        amp_ref[2 * shard_tiles:] = after_ref[...]
        fetch.wait()

    @pl.when(step * GROUP < live_ref[0])
    def _():
        for j in range(GROUP):
            slot = step * GROUP + j
            product = lax.dot_general(
                amp_ref[index_ref[slot]],
                block_ref[j],
                (((1,), (1,)), ((), ())),
                precision=lax.Precision.HIGHEST,
                preferred_element_type=jnp.float32,
            )
            target = index_ref[slots + slot]
            used = slot < live_ref[0]
            acc_ref[target] = acc_ref[target] + jnp.where(used, product, 0.0)

    @pl.when(step == pl.num_programs(0) - 1)
    def _():
        out_ref[...] = acc_ref[...]


def slot_products(index, live, before, own, after, blocks, tiles_ab):
    slots, block_width, width = blocks.shape
    pairs = own.shape[1]
    steps = slots // GROUP

    def block_map(i, *refs):
        last = jnp.maximum(refs[1][0] - 1, 0) // GROUP
        return (jnp.minimum(i, last), 0, 0)

    whole = lambda shape: pl.BlockSpec(shape, lambda i, *_: (0,) * len(shape))
    out_shape = (tiles_ab, pairs, block_width)
    grid_spec = pltpu.PrefetchScalarGridSpec(
        num_scalar_prefetch=2,
        grid=(steps,),
        in_specs=[
            whole(before.shape),
            pl.BlockSpec(memory_space=pltpu.HBM),
            whole(after.shape),
            pl.BlockSpec((GROUP, block_width, width), block_map),
        ],
        out_specs=whole(out_shape),
        scratch_shapes=[
            pltpu.VMEM((3 * own.shape[0],) + own.shape[1:], jnp.float32),
            pltpu.VMEM((tiles_ab, pairs, block_width), jnp.float32),
            pltpu.SemaphoreType.DMA((1,)),
        ],
    )
    return pl.pallas_call(
        slot_kernel,
        grid_spec=grid_spec,
        out_shape=jax.ShapeDtypeStruct(out_shape, jnp.float32),
        compiler_params=pltpu.CompilerParams(
            dimension_semantics=("arbitrary",), vmem_limit_bytes=48 * 1024 * 1024
        ),
        cost_estimate=pl.CostEstimate(
            flops=2 * slots * pairs * width * block_width * 6,
            bytes_accessed=4 * (slots * block_width * width + 3 * own.size + tiles_ab * pairs * block_width),
            transcendentals=0,
        ),
    )(index, live, before, own, after, blocks)


def exchange_rows(mirrored):
    size = lax.axis_size("row")
    index = lax.axis_index("row")
    width = mirrored.shape[1]
    received = [mirrored] + [
        lax.ppermute(mirrored, "row", [(i, (i + shift) % size) for i in range(size)])
        for shift in range(1, size)
    ]
    by_source = jnp.stack(received[::-1] + received[::-1], axis=0)
    start = (size - 1 - index) % size
    ordered = lax.dynamic_slice_in_dim(by_source, start, size, axis=0)
    columns = lax.dynamic_slice_in_dim(ordered, index * width, width, axis=3)
    return columns.reshape(1, size * width, width)


def shards(amplitudes, integrals, slot_ab, slot_cd, live_count, pair_list):
    tile_size = lax.axis_size(TILE)
    row_size = lax.axis_size("row")
    tile_index = lax.axis_index(TILE)
    core = lax.axis_index("c")
    cores = lax.axis_size("c")
    shard_tiles = amplitudes.shape[0]
    pair_count = amplitudes.shape[1]
    up = [(i, (i + 1) % tile_size) for i in range(tile_size)]
    down = [(j, i) for i, j in up]
    before = lax.ppermute(amplitudes, TILE, up)
    after = lax.ppermute(amplitudes, TILE, down)
    mirror = find_mirror(pair_list)
    chips_of = jnp.arange(pair_count // cores, dtype=jnp.int32) * cores
    kept = chips_of + core
    keep_rows = jnp.concatenate([kept, mirror[kept]])
    cd_global = slot_cd[0]
    owner_tile = cd_global // shard_tiles
    offset = (owner_tile - tile_index + 1 + tile_size) % tile_size
    a_tiles = SLAB // (row_size * ATS)
    b_tiles = SLAB // TS
    tiles_ab = a_tiles * b_tiles
    totals = slot_products(
        jnp.concatenate([offset * shard_tiles + cd_global % shard_tiles, slot_ab[0]]).astype(jnp.int32),
        live_count[0],
        before,
        amplitudes,
        after,
        integrals[0],
        tiles_ab,
    )
    pairs_axis = jnp.arange(pair_count, dtype=jnp.int32)[None, :]
    pick = lambda rows, source: jnp.einsum(
        "qp,epb->eqb",
        (rows[:, None] == pairs_axis).astype(jnp.float32),
        source,
        precision=lax.Precision.HIGHEST,
        preferred_element_type=jnp.float32,
    )
    both_cores = totals + lax.ppermute(totals, "c", [(0, 1), (1, 0)])
    summed = pick(keep_rows, both_cores)
    halves = summed.reshape(tiles_ab, 2, pair_count // cores, summed.shape[2])
    spread = lax.all_to_all(halves, CHIPS, 2, 2, tiled=True)
    reduced = jnp.sum(spread, axis=2)
    own = to_grid(reduced[:, 0][:, None], a_tiles, b_tiles)
    mirrored = to_grid(reduced[:, 1][:, None], a_tiles, b_tiles)
    turned = jnp.transpose(exchange_rows(mirrored), (0, 2, 1))
    return own + turned


def solution(mesh):
    tile_size = mesh.shape["tile"]
    row_size = mesh.shape["row"]
    cores = 2
    split = Mesh(
        mesh.devices.reshape(4, tile_size // (4 * cores), cores, row_size), ("x", "z", "c", "row")
    )
    return jax.shard_map(
        shards,
        mesh=split,
        in_specs=(
            P(TILE, None, None),
            P("row", TILE, None, None),
            P("row", TILE),
            P("row", TILE),
            P("row", TILE),
            P(),
        ),
        out_specs=P(TILE, "row", None),
        check_vma=False,
    )
```

```python
import functools

import jax
import jax.numpy as jnp
from jax import lax
from jax.experimental import pallas as pl
from jax.experimental.pallas import tpu as pltpu
from jax.sharding import Mesh, PartitionSpec as P

TS = 16
ATS = 8
SLAB = 96
GROUP = 32
CHIPS = ("x", "z")
TILE = ("x", "z", "c")


def padded(x, sides, width):
    for axis, dim in sides:
        size, length = (lax.axis_size(axis), x.shape[dim])
        up = [(i, (i + 1) % size) for i in range(size)]
        down = [(j, i) for i, j in up]
        last = lax.slice_in_dim(x, length - width, length, axis=dim)
        first = lax.slice_in_dim(x, 0, width, axis=dim)
        before = lax.ppermute(last, axis, up)
        after = lax.ppermute(first, axis, down)
        x = jnp.concatenate([before, x, after], axis=dim)
    return x


def find_mirror(pair_list):
    first_orb = pair_list[:, 0]
    second = pair_list[:, 1]
    matches = (first_orb[:, None] == second[None, :]) & (second[:, None] == first_orb[None, :])
    columns = jnp.arange(pair_list.shape[0], dtype=jnp.int32)
    return jnp.sum(jnp.where(matches, columns[None, :], 0), axis=1)


def to_grid(totals, a_tiles, b_tiles):
    pair_count = totals.shape[1]
    shaped = totals.reshape(a_tiles, b_tiles, pair_count, ATS, TS)
    return jnp.transpose(shaped, (2, 0, 3, 1, 4)).reshape(pair_count, a_tiles * ATS, b_tiles * TS)


def slot_kernel(index_ref, live_ref, before_ref, own_ref, after_ref,
                block_ref, out_ref, amp_ref, acc_ref, sem_ref):
    step = pl.program_id(0)
    shard_tiles = own_ref.shape[0]
    slots = index_ref.shape[0] // 2

    @pl.when(step == 0)
    def _():
        fetch = pltpu.make_async_copy(
            own_ref, amp_ref.at[shard_tiles:2 * shard_tiles], sem_ref.at[0]
        )
        fetch.start()
        acc_ref[...] = jnp.zeros_like(acc_ref)
        amp_ref[:shard_tiles] = before_ref[...]
        amp_ref[2 * shard_tiles:] = after_ref[...]
        fetch.wait()

    @pl.when(step * GROUP < live_ref[0])
    def _():
        for j in range(GROUP):
            slot = step * GROUP + j
            product = lax.dot_general(
                amp_ref[index_ref[slot]],
                block_ref[j],
                (((1,), (1,)), ((), ())),
                precision=lax.Precision.HIGHEST,
                preferred_element_type=jnp.float32,
            )
            target = index_ref[slots + slot]
            used = slot < live_ref[0]
            acc_ref[target] = acc_ref[target] + jnp.where(used, product, 0.0)

    @pl.when(step == pl.num_programs(0) - 1)
    def _():
        out_ref[...] = acc_ref[...]


def slot_products(index, live, before, own, after, blocks, tiles_ab):
    slots, block_width, width = blocks.shape
    pairs = own.shape[1]
    steps = slots // GROUP

    def block_map(i, *refs):
        last = jnp.maximum(refs[1][0] - 1, 0) // GROUP
        return (jnp.minimum(i, last), 0, 0)

    whole = lambda shape: pl.BlockSpec(shape, lambda i, *_: (0,) * len(shape))
    out_shape = (tiles_ab, pairs, block_width)
    grid_spec = pltpu.PrefetchScalarGridSpec(
        num_scalar_prefetch=2,
        grid=(steps,),
        in_specs=[
            whole(before.shape),
            pl.BlockSpec(memory_space=pltpu.HBM),
            whole(after.shape),
            pl.BlockSpec((GROUP, block_width, width), block_map),
        ],
        out_specs=whole(out_shape),
        scratch_shapes=[
            pltpu.VMEM((3 * own.shape[0],) + own.shape[1:], jnp.float32),
            pltpu.VMEM((tiles_ab, pairs, block_width), jnp.float32),
            pltpu.SemaphoreType.DMA((1,)),
        ],
    )
    return pl.pallas_call(
        slot_kernel,
        grid_spec=grid_spec,
        out_shape=jax.ShapeDtypeStruct(out_shape, jnp.float32),
        compiler_params=pltpu.CompilerParams(
            dimension_semantics=("arbitrary",), vmem_limit_bytes=48 * 1024 * 1024
        ),
        cost_estimate=pl.CostEstimate(
            flops=2 * slots * pairs * width * block_width * 6,
            bytes_accessed=4 * (slots * block_width * width + 3 * own.size + tiles_ab * pairs * block_width),
            transcendentals=0,
        ),
    )(index, live, before, own, after, blocks)


def exchange_rows(mirrored):
    size = lax.axis_size("row")
    index = lax.axis_index("row")
    width = mirrored.shape[1]
    received = [mirrored] + [
        lax.ppermute(mirrored, "row", [(i, (i + shift) % size) for i in range(size)])
        for shift in range(1, size)
    ]
    by_source = jnp.stack(received[::-1] + received[::-1], axis=0)
    start = (size - 1 - index) % size
    ordered = lax.dynamic_slice_in_dim(by_source, start, size, axis=0)
    columns = lax.dynamic_slice_in_dim(ordered, index * width, width, axis=3)
    return columns.reshape(1, size * width, width)


def shards(amplitudes, integrals, slot_ab, slot_cd, live_count, pair_list):
    tile_size = lax.axis_size(TILE)
    row_size = lax.axis_size("row")
    tile_index = lax.axis_index(TILE)
    core = lax.axis_index("c")
    cores = lax.axis_size("c")
    shard_tiles = amplitudes.shape[0]
    pair_count = amplitudes.shape[1]
    up = [(i, (i + 1) % tile_size) for i in range(tile_size)]
    down = [(j, i) for i, j in up]
    before = lax.ppermute(amplitudes, TILE, up)
    after = lax.ppermute(amplitudes, TILE, down)
    mirror = find_mirror(pair_list)
    chips_of = jnp.arange(pair_count // cores, dtype=jnp.int32) * cores
    kept = chips_of + core
    keep_rows = jnp.concatenate([kept, mirror[kept]])
    cd_global = slot_cd[0]
    owner_tile = cd_global // shard_tiles
    offset = (owner_tile - tile_index + 1 + tile_size) % tile_size
    a_tiles = SLAB // (row_size * ATS)
    b_tiles = SLAB // TS
    tiles_ab = a_tiles * b_tiles
    totals = slot_products(
        jnp.concatenate([offset * shard_tiles + cd_global % shard_tiles, slot_ab[0]]).astype(jnp.int32),
        live_count[0],
        before,
        amplitudes,
        after,
        integrals[0],
        tiles_ab,
    )
    pairs_axis = jnp.arange(pair_count, dtype=jnp.int32)[None, :]
    pick = lambda rows, source: jnp.einsum(
        "qp,epb->eqb",
        (rows[:, None] == pairs_axis).astype(jnp.float32),
        source,
        precision=lax.Precision.HIGHEST,
        preferred_element_type=jnp.float32,
    )
    both_cores = totals + lax.ppermute(totals, "c", [(0, 1), (1, 0)])
    summed = pick(keep_rows, both_cores)
    halves = summed.reshape(tiles_ab, 2, pair_count // cores, summed.shape[2])
    spread = lax.all_to_all(halves, CHIPS, 2, 2, tiled=True)
    reduced = jnp.sum(spread, axis=2)
    own = to_grid(reduced[:, 0][:, None], a_tiles, b_tiles)
    mirrored = to_grid(reduced[:, 1][:, None], a_tiles, b_tiles)
    turned = jnp.transpose(exchange_rows(mirrored), (0, 2, 1))
    return own + turned


def solution(mesh):
    tile_size = mesh.shape["tile"]
    row_size = mesh.shape["row"]
    cores = 2
    split = Mesh(
        mesh.devices.reshape(4, tile_size // (4 * cores), cores, row_size), ("x", "z", "c", "row")
    )
    return jax.shard_map(
        shards,
        mesh=split,
        in_specs=(
            P(TILE, None, None),
            P("row", TILE, None, None),
            P("row", TILE),
            P("row", TILE),
            P("row", TILE),
            P(),
        ),
        out_specs=P(TILE, "row", None),
        check_vma=False,
    )
```

```python
import functools

import jax
import jax.numpy as jnp
from jax import lax
from jax.experimental import pallas as pl
from jax.experimental.pallas import tpu as pltpu
from jax.sharding import Mesh, PartitionSpec as P

TS = 16
ATS = 8
SLAB = 96
GROUP = 16
CHIPS = ("x", "z")
TILE = ("x", "z", "c")


def padded(x, sides, width):
    for axis, dim in sides:
        size, length = (lax.axis_size(axis), x.shape[dim])
        up = [(i, (i + 1) % size) for i in range(size)]
        down = [(j, i) for i, j in up]
        last = lax.slice_in_dim(x, length - width, length, axis=dim)
        first = lax.slice_in_dim(x, 0, width, axis=dim)
        before = lax.ppermute(last, axis, up)
        after = lax.ppermute(first, axis, down)
        x = jnp.concatenate([before, x, after], axis=dim)
    return x


def find_mirror(pair_list):
    first_orb = pair_list[:, 0]
    second = pair_list[:, 1]
    matches = (first_orb[:, None] == second[None, :]) & (second[:, None] == first_orb[None, :])
    columns = jnp.arange(pair_list.shape[0], dtype=jnp.int32)
    return jnp.sum(jnp.where(matches, columns[None, :], 0), axis=1)


def to_grid(totals, a_tiles, b_tiles):
    pair_count = totals.shape[1]
    shaped = totals.reshape(a_tiles, b_tiles, pair_count, ATS, TS)
    return jnp.transpose(shaped, (2, 0, 3, 1, 4)).reshape(pair_count, a_tiles * ATS, b_tiles * TS)


def slot_kernel(index_ref, live_ref, before_ref, own_ref, after_ref,
                block_ref, out_ref, amp_ref, acc_ref, sem_ref):
    step = pl.program_id(0)
    shard_tiles = own_ref.shape[0]
    slots = index_ref.shape[0] // 2

    @pl.when(step == 0)
    def _():
        fetch = pltpu.make_async_copy(
            own_ref, amp_ref.at[shard_tiles:2 * shard_tiles], sem_ref.at[0]
        )
        fetch.start()
        acc_ref[...] = jnp.zeros_like(acc_ref)
        amp_ref[:shard_tiles] = before_ref[...]
        amp_ref[2 * shard_tiles:] = after_ref[...]
        fetch.wait()

    @pl.when(step * GROUP < live_ref[0])
    def _():
        for j in range(GROUP):
            slot = step * GROUP + j
            product = lax.dot_general(
                block_ref[j],
                amp_ref[index_ref[slot]],
                (((1,), (1,)), ((), ())),
                precision=lax.Precision.HIGHEST,
                preferred_element_type=jnp.float32,
            )
            target = index_ref[slots + slot]
            used = slot < live_ref[0]
            acc_ref[target] = acc_ref[target] + jnp.where(used, product, 0.0)

    @pl.when(step == pl.num_programs(0) - 1)
    def _():
        out_ref[...] = acc_ref[...]


def slot_products(index, live, before, own, after, blocks, tiles_ab):
    slots, block_width, width = blocks.shape
    pairs = own.shape[1]
    steps = slots // GROUP

    def block_map(i, *refs):
        last = jnp.maximum(refs[1][0] - 1, 0) // GROUP
        return (jnp.minimum(i, last), 0, 0)

    whole = lambda shape: pl.BlockSpec(shape, lambda i, *_: (0,) * len(shape))
    out_shape = (tiles_ab, block_width, pairs)
    grid_spec = pltpu.PrefetchScalarGridSpec(
        num_scalar_prefetch=2,
        grid=(steps,),
        in_specs=[
            whole(before.shape),
            pl.BlockSpec(memory_space=pltpu.HBM),
            whole(after.shape),
            pl.BlockSpec((GROUP, block_width, width), block_map),
        ],
        out_specs=whole(out_shape),
        scratch_shapes=[
            pltpu.VMEM((3 * own.shape[0],) + own.shape[1:], jnp.float32),
            pltpu.VMEM((tiles_ab, block_width, pairs), jnp.float32),
            pltpu.SemaphoreType.DMA((1,)),
        ],
    )
    return pl.pallas_call(
        slot_kernel,
        grid_spec=grid_spec,
        out_shape=jax.ShapeDtypeStruct(out_shape, jnp.float32),
        compiler_params=pltpu.CompilerParams(
            dimension_semantics=("arbitrary",), vmem_limit_bytes=48 * 1024 * 1024
        ),
        cost_estimate=pl.CostEstimate(
            flops=2 * slots * pairs * width * block_width * 6,
            bytes_accessed=4 * (slots * block_width * width + 3 * own.size + tiles_ab * pairs * block_width),
            transcendentals=0,
        ),
    )(index, live, before, own, after, blocks)


def exchange_rows(mirrored):
    size = lax.axis_size("row")
    index = lax.axis_index("row")
    width = mirrored.shape[1]
    received = [mirrored] + [
        lax.ppermute(mirrored, "row", [(i, (i + shift) % size) for i in range(size)])
        for shift in range(1, size)
    ]
    by_source = jnp.stack(received[::-1] + received[::-1], axis=0)
    start = (size - 1 - index) % size
    ordered = lax.dynamic_slice_in_dim(by_source, start, size, axis=0)
    columns = lax.dynamic_slice_in_dim(ordered, index * width, width, axis=3)
    return columns.reshape(1, size * width, width)


def shards(amplitudes, integrals, slot_ab, slot_cd, live_count, pair_list):
    tile_size = lax.axis_size(TILE)
    row_size = lax.axis_size("row")
    tile_index = lax.axis_index(TILE)
    core = lax.axis_index("c")
    cores = lax.axis_size("c")
    shard_tiles = amplitudes.shape[0]
    pair_count = amplitudes.shape[1]
    up = [(i, (i + 1) % tile_size) for i in range(tile_size)]
    down = [(j, i) for i, j in up]
    before = lax.ppermute(amplitudes, TILE, up)
    after = lax.ppermute(amplitudes, TILE, down)
    mirror = find_mirror(pair_list)
    chips_of = jnp.arange(pair_count // cores, dtype=jnp.int32) * cores
    kept = chips_of + core
    keep_rows = jnp.concatenate([kept, mirror[kept]])
    cd_global = slot_cd[0]
    owner_tile = cd_global // shard_tiles
    offset = (owner_tile - tile_index + 1 + tile_size) % tile_size
    a_tiles = SLAB // (row_size * ATS)
    b_tiles = SLAB // TS
    tiles_ab = a_tiles * b_tiles
    totals = slot_products(
        jnp.concatenate([offset * shard_tiles + cd_global % shard_tiles, slot_ab[0]]).astype(jnp.int32),
        live_count[0],
        before,
        amplitudes,
        after,
        integrals[0],
        tiles_ab,
    )
    pairs_axis = jnp.arange(pair_count, dtype=jnp.int32)[None, :]
    pick = lambda rows, source: jnp.einsum(
        "qp,ebp->eqb",
        (rows[:, None] == pairs_axis).astype(jnp.float32),
        source,
        precision=lax.Precision.HIGHEST,
        preferred_element_type=jnp.float32,
    )
    both_cores = totals + lax.ppermute(totals, "c", [(0, 1), (1, 0)])
    summed = pick(keep_rows, both_cores)
    halves = summed.reshape(tiles_ab, 2, pair_count // cores, summed.shape[2])
    spread = lax.all_to_all(halves, CHIPS, 2, 2, tiled=True)
    reduced = jnp.sum(spread, axis=2)
    own = to_grid(reduced[:, 0][:, None], a_tiles, b_tiles)
    mirrored = to_grid(reduced[:, 1][:, None], a_tiles, b_tiles)
    turned = jnp.transpose(exchange_rows(mirrored), (0, 2, 1))
    return own + turned


def solution(mesh):
    tile_size = mesh.shape["tile"]
    row_size = mesh.shape["row"]
    cores = 2
    split = Mesh(
        mesh.devices.reshape(4, tile_size // (4 * cores), cores, row_size), ("x", "z", "c", "row")
    )
    return jax.shard_map(
        shards,
        mesh=split,
        in_specs=(
            P(TILE, None, None),
            P("row", TILE, None, None),
            P("row", TILE),
            P("row", TILE),
            P("row", TILE),
            P(),
        ),
        out_specs=P(TILE, "row", None),
        check_vma=False,
    )
```

```python
import functools

import jax
import jax.numpy as jnp
from jax import lax
from jax.experimental import pallas as pl
from jax.experimental.pallas import tpu as pltpu
from jax.sharding import Mesh, PartitionSpec as P

TS = 16
ATS = 8
SLAB = 96
GROUP = 32
CHIPS = ("x", "z")
TILE = ("x", "z", "c")


def padded(x, sides, width):
    for axis, dim in sides:
        size, length = (lax.axis_size(axis), x.shape[dim])
        up = [(i, (i + 1) % size) for i in range(size)]
        down = [(j, i) for i, j in up]
        last = lax.slice_in_dim(x, length - width, length, axis=dim)
        first = lax.slice_in_dim(x, 0, width, axis=dim)
        before = lax.ppermute(last, axis, up)
        after = lax.ppermute(first, axis, down)
        x = jnp.concatenate([before, x, after], axis=dim)
    return x


def find_mirror(pair_list):
    first_orb = pair_list[:, 0]
    second = pair_list[:, 1]
    matches = (first_orb[:, None] == second[None, :]) & (second[:, None] == first_orb[None, :])
    columns = jnp.arange(pair_list.shape[0], dtype=jnp.int32)
    return jnp.sum(jnp.where(matches, columns[None, :], 0), axis=1)


def to_grid(totals, a_tiles, b_tiles):
    pair_count = totals.shape[1]
    shaped = totals.reshape(a_tiles, b_tiles, pair_count, ATS, TS)
    return jnp.transpose(shaped, (2, 0, 3, 1, 4)).reshape(pair_count, a_tiles * ATS, b_tiles * TS)


def slot_kernel(index_ref, live_ref, before_ref, own_ref, after_ref,
                block_ref, out_ref, amp_ref, acc_ref, sem_ref):
    step = pl.program_id(0)
    shard_tiles = own_ref.shape[0]
    slots = index_ref.shape[0] // 2

    @pl.when(step == 0)
    def _():
        fetch = pltpu.make_async_copy(
            own_ref, amp_ref.at[shard_tiles:2 * shard_tiles], sem_ref.at[0]
        )
        fetch.start()
        acc_ref[...] = jnp.zeros_like(acc_ref)
        amp_ref[:shard_tiles] = before_ref[...]
        amp_ref[2 * shard_tiles:] = after_ref[...]
        fetch.wait()

    @pl.when(step * GROUP < live_ref[0])
    def _():
        for j in range(GROUP):
            slot = step * GROUP + j
            product = lax.dot_general(
                block_ref[j],
                amp_ref[index_ref[slot]],
                (((1,), (1,)), ((), ())),
                precision=lax.Precision.HIGHEST,
                preferred_element_type=jnp.float32,
            )
            target = index_ref[slots + slot]
            used = slot < live_ref[0]
            acc_ref[target] = acc_ref[target] + jnp.where(used, product, 0.0)

    @pl.when(step == pl.num_programs(0) - 1)
    def _():
        out_ref[...] = acc_ref[...]


def slot_products(index, live, before, own, after, blocks, tiles_ab):
    slots, block_width, width = blocks.shape
    pairs = own.shape[1]
    steps = slots // GROUP

    def block_map(i, *refs):
        last = jnp.maximum(refs[1][0] - 1, 0) // GROUP
        return (jnp.minimum(i, last), 0, 0)

    whole = lambda shape: pl.BlockSpec(shape, lambda i, *_: (0,) * len(shape))
    out_shape = (tiles_ab, block_width, pairs)
    grid_spec = pltpu.PrefetchScalarGridSpec(
        num_scalar_prefetch=2,
        grid=(steps,),
        in_specs=[
            whole(before.shape),
            pl.BlockSpec(memory_space=pltpu.HBM),
            whole(after.shape),
            pl.BlockSpec((GROUP, block_width, width), block_map),
        ],
        out_specs=whole(out_shape),
        scratch_shapes=[
            pltpu.VMEM((3 * own.shape[0],) + own.shape[1:], jnp.float32),
            pltpu.VMEM((tiles_ab, block_width, pairs), jnp.float32),
            pltpu.SemaphoreType.DMA((1,)),
        ],
    )
    return pl.pallas_call(
        slot_kernel,
        grid_spec=grid_spec,
        out_shape=jax.ShapeDtypeStruct(out_shape, jnp.float32),
        compiler_params=pltpu.CompilerParams(
            dimension_semantics=("arbitrary",), vmem_limit_bytes=48 * 1024 * 1024
        ),
        cost_estimate=pl.CostEstimate(
            flops=2 * slots * pairs * width * block_width * 6,
            bytes_accessed=4 * (slots * block_width * width + 3 * own.size + tiles_ab * pairs * block_width),
            transcendentals=0,
        ),
    )(index, live, before, own, after, blocks)


def exchange_rows(mirrored):
    size = lax.axis_size("row")
    index = lax.axis_index("row")
    width = mirrored.shape[1]
    received = [mirrored] + [
        lax.ppermute(mirrored, "row", [(i, (i + shift) % size) for i in range(size)])
        for shift in range(1, size)
    ]
    by_source = jnp.stack(received[::-1] + received[::-1], axis=0)
    start = (size - 1 - index) % size
    ordered = lax.dynamic_slice_in_dim(by_source, start, size, axis=0)
    columns = lax.dynamic_slice_in_dim(ordered, index * width, width, axis=3)
    return columns.reshape(1, size * width, width)


def shards(amplitudes, integrals, slot_ab, slot_cd, live_count, pair_list):
    tile_size = lax.axis_size(TILE)
    row_size = lax.axis_size("row")
    tile_index = lax.axis_index(TILE)
    core = lax.axis_index("c")
    cores = lax.axis_size("c")
    shard_tiles = amplitudes.shape[0]
    pair_count = amplitudes.shape[1]
    up = [(i, (i + 1) % tile_size) for i in range(tile_size)]
    down = [(j, i) for i, j in up]
    before = lax.ppermute(amplitudes, TILE, up)
    after = lax.ppermute(amplitudes, TILE, down)
    mirror = find_mirror(pair_list)
    chips_of = jnp.arange(pair_count // cores, dtype=jnp.int32) * cores
    kept = chips_of + core
    keep_rows = jnp.concatenate([kept, mirror[kept]])
    cd_global = slot_cd[0]
    owner_tile = cd_global // shard_tiles
    offset = (owner_tile - tile_index + 1 + tile_size) % tile_size
    a_tiles = SLAB // (row_size * ATS)
    b_tiles = SLAB // TS
    tiles_ab = a_tiles * b_tiles
    totals = slot_products(
        jnp.concatenate([offset * shard_tiles + cd_global % shard_tiles, slot_ab[0]]).astype(jnp.int32),
        live_count[0],
        before,
        amplitudes,
        after,
        integrals[0],
        tiles_ab,
    )
    pairs_axis = jnp.arange(pair_count, dtype=jnp.int32)[None, :]
    pick = lambda rows, source: jnp.einsum(
        "qp,ebp->eqb",
        (rows[:, None] == pairs_axis).astype(jnp.float32),
        source,
        precision=lax.Precision.HIGHEST,
        preferred_element_type=jnp.float32,
    )
    both_cores = totals + lax.ppermute(totals, "c", [(0, 1), (1, 0)])
    summed = pick(keep_rows, both_cores)
    halves = summed.reshape(tiles_ab, 2, pair_count // cores, summed.shape[2])
    spread = lax.all_to_all(halves, CHIPS, 2, 2, tiled=True)
    reduced = jnp.sum(spread, axis=2)
    own = to_grid(reduced[:, 0][:, None], a_tiles, b_tiles)
    mirrored = to_grid(reduced[:, 1][:, None], a_tiles, b_tiles)
    turned = jnp.transpose(exchange_rows(mirrored), (0, 2, 1))
    return own + turned


def solution(mesh):
    tile_size = mesh.shape["tile"]
    row_size = mesh.shape["row"]
    cores = 2
    split = Mesh(
        mesh.devices.reshape(4, tile_size // (4 * cores), cores, row_size), ("x", "z", "c", "row")
    )
    return jax.shard_map(
        shards,
        mesh=split,
        in_specs=(
            P(TILE, None, None),
            P("row", TILE, None, None),
            P("row", TILE),
            P("row", TILE),
            P("row", TILE),
            P(),
        ),
        out_specs=P(TILE, "row", None),
        check_vma=False,
    )
```

```python
import functools

import jax
import jax.numpy as jnp
from jax import lax
from jax.experimental import pallas as pl
from jax.experimental.pallas import tpu as pltpu
from jax.sharding import Mesh, PartitionSpec as P

TS = 16
ATS = 8
SLAB = 96
GROUP = 8
CHIPS = ("x", "z")
TILE = ("x", "z", "c")


def padded(x, sides, width):
    for axis, dim in sides:
        size, length = (lax.axis_size(axis), x.shape[dim])
        up = [(i, (i + 1) % size) for i in range(size)]
        down = [(j, i) for i, j in up]
        last = lax.slice_in_dim(x, length - width, length, axis=dim)
        first = lax.slice_in_dim(x, 0, width, axis=dim)
        before = lax.ppermute(last, axis, up)
        after = lax.ppermute(first, axis, down)
        x = jnp.concatenate([before, x, after], axis=dim)
    return x


def find_mirror(pair_list):
    first_orb = pair_list[:, 0]
    second = pair_list[:, 1]
    matches = (first_orb[:, None] == second[None, :]) & (second[:, None] == first_orb[None, :])
    columns = jnp.arange(pair_list.shape[0], dtype=jnp.int32)
    return jnp.sum(jnp.where(matches, columns[None, :], 0), axis=1)


def to_grid(totals, a_tiles, b_tiles):
    pair_count = totals.shape[1]
    shaped = totals.reshape(a_tiles, b_tiles, pair_count, ATS, TS)
    return jnp.transpose(shaped, (2, 0, 3, 1, 4)).reshape(pair_count, a_tiles * ATS, b_tiles * TS)


def slot_kernel(index_ref, live_ref, before_ref, own_ref, after_ref,
                block_ref, out_ref, amp_ref, acc_ref, sem_ref):
    step = pl.program_id(0)
    shard_tiles = own_ref.shape[0]
    slots = index_ref.shape[0] // 2

    @pl.when(step == 0)
    def _():
        fetch = pltpu.make_async_copy(
            own_ref, amp_ref.at[shard_tiles:2 * shard_tiles], sem_ref.at[0]
        )
        fetch.start()
        acc_ref[...] = jnp.zeros_like(acc_ref)
        amp_ref[:shard_tiles] = before_ref[...]
        amp_ref[2 * shard_tiles:] = after_ref[...]
        fetch.wait()

    @pl.when(step * GROUP < live_ref[0])
    def _():
        for j in range(GROUP):
            slot = step * GROUP + j
            product = lax.dot_general(
                block_ref[j],
                amp_ref[index_ref[slot]],
                (((1,), (1,)), ((), ())),
                precision=lax.Precision.HIGHEST,
                preferred_element_type=jnp.float32,
            )
            target = index_ref[slots + slot]
            used = slot < live_ref[0]
            acc_ref[target] = acc_ref[target] + jnp.where(used, product, 0.0)

    @pl.when(step == pl.num_programs(0) - 1)
    def _():
        out_ref[...] = acc_ref[...]


def slot_products(index, live, before, own, after, blocks, tiles_ab):
    slots, block_width, width = blocks.shape
    pairs = own.shape[1]
    steps = slots // GROUP

    def block_map(i, *refs):
        last = jnp.maximum(refs[1][0] - 1, 0) // GROUP
        return (jnp.minimum(i, last), 0, 0)

    whole = lambda shape: pl.BlockSpec(shape, lambda i, *_: (0,) * len(shape))
    out_shape = (tiles_ab, block_width, pairs)
    grid_spec = pltpu.PrefetchScalarGridSpec(
        num_scalar_prefetch=2,
        grid=(steps,),
        in_specs=[
            whole(before.shape),
            pl.BlockSpec(memory_space=pltpu.HBM),
            whole(after.shape),
            pl.BlockSpec((GROUP, block_width, width), block_map),
        ],
        out_specs=whole(out_shape),
        scratch_shapes=[
            pltpu.VMEM((3 * own.shape[0],) + own.shape[1:], jnp.float32),
            pltpu.VMEM((tiles_ab, block_width, pairs), jnp.float32),
            pltpu.SemaphoreType.DMA((1,)),
        ],
    )
    return pl.pallas_call(
        slot_kernel,
        grid_spec=grid_spec,
        out_shape=jax.ShapeDtypeStruct(out_shape, jnp.float32),
        compiler_params=pltpu.CompilerParams(
            dimension_semantics=("arbitrary",), vmem_limit_bytes=48 * 1024 * 1024
        ),
        cost_estimate=pl.CostEstimate(
            flops=2 * slots * pairs * width * block_width * 6,
            bytes_accessed=4 * (slots * block_width * width + 3 * own.size + tiles_ab * pairs * block_width),
            transcendentals=0,
        ),
    )(index, live, before, own, after, blocks)


def exchange_rows(mirrored):
    size = lax.axis_size("row")
    index = lax.axis_index("row")
    width = mirrored.shape[1]
    received = [mirrored] + [
        lax.ppermute(mirrored, "row", [(i, (i + shift) % size) for i in range(size)])
        for shift in range(1, size)
    ]
    by_source = jnp.stack(received[::-1] + received[::-1], axis=0)
    start = (size - 1 - index) % size
    ordered = lax.dynamic_slice_in_dim(by_source, start, size, axis=0)
    columns = lax.dynamic_slice_in_dim(ordered, index * width, width, axis=3)
    return columns.reshape(1, size * width, width)


def shards(amplitudes, integrals, slot_ab, slot_cd, live_count, pair_list):
    tile_size = lax.axis_size(TILE)
    row_size = lax.axis_size("row")
    tile_index = lax.axis_index(TILE)
    core = lax.axis_index("c")
    cores = lax.axis_size("c")
    shard_tiles = amplitudes.shape[0]
    pair_count = amplitudes.shape[1]
    up = [(i, (i + 1) % tile_size) for i in range(tile_size)]
    down = [(j, i) for i, j in up]
    before = lax.ppermute(amplitudes, TILE, up)
    after = lax.ppermute(amplitudes, TILE, down)
    mirror = find_mirror(pair_list)
    chips_of = jnp.arange(pair_count // cores, dtype=jnp.int32) * cores
    kept = chips_of + core
    keep_rows = jnp.concatenate([kept, mirror[kept]])
    cd_global = slot_cd[0]
    owner_tile = cd_global // shard_tiles
    offset = (owner_tile - tile_index + 1 + tile_size) % tile_size
    a_tiles = SLAB // (row_size * ATS)
    b_tiles = SLAB // TS
    tiles_ab = a_tiles * b_tiles
    totals = slot_products(
        jnp.concatenate([offset * shard_tiles + cd_global % shard_tiles, slot_ab[0]]).astype(jnp.int32),
        live_count[0],
        before,
        amplitudes,
        after,
        integrals[0],
        tiles_ab,
    )
    pairs_axis = jnp.arange(pair_count, dtype=jnp.int32)[None, :]
    pick = lambda rows, source: jnp.einsum(
        "qp,ebp->eqb",
        (rows[:, None] == pairs_axis).astype(jnp.float32),
        source,
        precision=lax.Precision.HIGHEST,
        preferred_element_type=jnp.float32,
    )
    both_cores = totals + lax.ppermute(totals, "c", [(0, 1), (1, 0)])
    summed = pick(keep_rows, both_cores)
    halves = summed.reshape(tiles_ab, 2, pair_count // cores, summed.shape[2])
    spread = lax.all_to_all(halves, CHIPS, 2, 2, tiled=True)
    reduced = jnp.sum(spread, axis=2)
    own = to_grid(reduced[:, 0][:, None], a_tiles, b_tiles)
    mirrored = to_grid(reduced[:, 1][:, None], a_tiles, b_tiles)
    turned = jnp.transpose(exchange_rows(mirrored), (0, 2, 1))
    return own + turned


def solution(mesh):
    tile_size = mesh.shape["tile"]
    row_size = mesh.shape["row"]
    cores = 2
    split = Mesh(
        mesh.devices.reshape(4, tile_size // (4 * cores), cores, row_size), ("x", "z", "c", "row")
    )
    return jax.shard_map(
        shards,
        mesh=split,
        in_specs=(
            P(TILE, None, None),
            P("row", TILE, None, None),
            P("row", TILE),
            P("row", TILE),
            P("row", TILE),
            P(),
        ),
        out_specs=P(TILE, "row", None),
        check_vma=False,
    )
```
